256 devices in a mesh: row: 4 (over y), col: 4 (over x), dp: 16 (over z, core).
Axes of the slice: x: 4, y: 4, z: 8, core: 2. Of those that a mesh axis runs over, the one named last changes fastest.
Arguments:
- hidden_states: bfloat16 [16384, 1536], P(('dp', 'row'), 'col'), may hold values from -18 to 18
- w_query: bfloat16 [1536, 1536], P('col', 'row'), may hold values from -0.102062073 to 0.102062073
- w_key_value: bfloat16 [1536, 512], P('col'), may hold values from -0.102062073 to 0.102062073
- adapter_down: bfloat16 [1024, 1536, 16], P('dp', 'col'), may hold values from -0.15625 to 0.15625
- adapter_up: bfloat16 [1024, 16, 1536], P('dp', None, 'row'), may hold values from -1.5 to 1.5
- req_lengths: int32 [16, 8], replicated, may hold values from 1 to 160, 960 in all within a row
- req_adapter: int32 [16, 8], replicated, may hold values from 0 to 1023, as said below
Outputs:
- attention: bfloat16 [16384, 1536], P(('dp', 'col'), 'row')
- kv_cache: bfloat16 [16384, 512], P(('dp', 'col'))
The draws below stay inside these ranges and needn't reach their ends.
Inputs may be any that keep to these rules, and one draw needn't show every extreme that they name: `req_lengths`: the lengths of one block sum to 960, and each block has a request of exactly 160 tokens. `req_adapter`: adapters k * 64 to (k + 1) * 64 - 1 are those of index k of dp; the requests of one block use adapters of one index of dp at most 1 times, and some index of dp is used exactly that often by every block.
All inputs are finite; a program needn't handle non-finite values.
Results may differ from the reference program's by a relative error of at most 0.0072.
Values may be sent and summed in bfloat16 or wider, within the bound.
No kernel may reach another device: no remote copies, remote signals or barrier semaphores. Data moves between devices by JAX's collectives and lax.ppermute only.
A program may use at most 128 MiB of HBM per device.

```python
import math
import jax
import jax.numpy as jnp
import numpy as np
from jax import lax

D = 1536
HEADS = 12
KV_HEADS = 2
HEAD_DIM = 128
RANK = 16
ADP_DEV = 64
GROUP_TOK = 1024
PREFIX = 64
REQ_DEV = 8
MOST_LEN = 160
ADAPTERS = 1024
TOKENS = 16384
N_DP = 16


def draw_hidden_states(key, part):
    base_key = jax.random.fold_in(key, 7)
    drawn_rows = jnp.clip(jax.random.normal(jax.random.fold_in(base_key, 1), (TOKENS, D), jnp.float32), -6.0, 6.0)
    return drawn_rows.astype(jnp.bfloat16)


def weight_pair(key):
    base_key = jax.random.fold_in(key, 101)
    key_cols = jnp.clip(jax.random.normal(jax.random.fold_in(base_key, 1), (D, KV_HEADS * HEAD_DIM), jnp.float32), -4.0, 4.0) / math.sqrt(D)
    value_cols = jnp.clip(jax.random.normal(jax.random.fold_in(base_key, 2), (D, KV_HEADS * HEAD_DIM), jnp.float32), -4.0, 4.0) / math.sqrt(D)
    noise_cols = jnp.clip(jax.random.normal(jax.random.fold_in(base_key, 3), (D, HEADS * HEAD_DIM), jnp.float32), -4.0, 4.0) / math.sqrt(D)
    query_cols = noise_cols
    return (query_cols, jnp.concatenate([key_cols, value_cols], axis=1))


def draw_w_query(key, part):
    return weight_pair(key)[0].astype(jnp.bfloat16)


def draw_w_key_value(key, part):
    return weight_pair(key)[1].astype(jnp.bfloat16)


def draw_req_adapter(key, part):
    base_key = jax.random.fold_in(key, 13)
    offset_dp = jax.random.randint(jax.random.fold_in(base_key, 1), (), 0, N_DP)
    block_keys = jax.random.split(jax.random.fold_in(base_key, 2), N_DP)

    def block_ids(block_key):
        other_ids = jax.random.permutation(jax.random.fold_in(block_key, 1), N_DP - 1).astype(jnp.int32) + 1
        cycle_ids = jnp.concatenate([jnp.zeros((1,), jnp.int32), other_ids])
        req_order = jax.random.permutation(jax.random.fold_in(block_key, 2), REQ_DEV).astype(jnp.int32)
        holder_ids = (cycle_ids[req_order % N_DP] + offset_dp) % N_DP
        adapter_pick = jax.random.randint(jax.random.fold_in(block_key, 3), (REQ_DEV,), 0, ADP_DEV)
        return (holder_ids * ADP_DEV + adapter_pick).astype(jnp.int32)
    return jax.vmap(block_ids)(block_keys)


def shard_levels(own_key, dims, cuts, low, high):
    level = 1.0
    for position, shards_of in cuts:
        heights = jax.random.uniform(jax.random.fold_in(jax.random.fold_in(own_key, 6), position), (shards_of,), jnp.float32, low / len(cuts), high / len(cuts))
        level = level * jnp.repeat(jnp.exp(heights), dims[position] // shards_of).reshape((-1,) + (1,) * (len(dims) - 1 - position))
    return level


def length_profile(number_of, total, most, slope):
    loads = [(1 << 20) // math.isqrt(standing ** slope) + 1 for standing in range(2, number_of + 1)]
    surplus, holding = total - most - (number_of - 1), [1] * (number_of - 1)
    while surplus > 0:
        movable = [i for i in range(number_of - 1) if holding[i] < most]
        pool, budget = sum([loads[i] for i in movable]), surplus
        for i in movable:
            addition = min(most - holding[i], max(1, budget * loads[i] // pool), surplus)
            holding[i] = holding[i] + addition
            surplus = surplus - addition
    return np.array([most] + holding)


def uneven(stream_key, number_of, total, reach, slope):
    if number_of == 2:
        one = jax.random.randint(stream_key, (), max(1, total - reach), min(reach, total - 1) + 1)
        return jnp.stack([one, total - one])
    tallies = jnp.asarray(length_profile(number_of, total, reach, slope), jnp.int32)
    pairs = (number_of - 1) // 2
    giver, sink = tallies[1:1 + 2 * pairs:2], tallies[2:2 + 2 * pairs:2]
    slack = jnp.minimum(giver - 1, reach - sink)
    passed = jax.random.randint(jax.random.fold_in(stream_key, 1), (pairs,), 0, 1 << 20) % (slack + 1)
    tallies = tallies.at[1:1 + 2 * pairs:2].set(giver - passed).at[2:2 + 2 * pairs:2].set(sink + passed)
    return tallies[jax.random.permutation(jax.random.fold_in(stream_key, 2), number_of)]


def bell_draw(rng, dims, width, reach, shards=(), kind=jnp.bfloat16):
    result = width * jax.random.normal(rng, dims, jnp.float32)
    if shards:
        result = result * shard_levels(rng, dims, shards, -0.22, 0.18)
    return jnp.clip(result, -reach, reach).astype(kind)


def setup_inputs(seed: int = 0) -> dict:
    splits = jax.random.split(jax.random.key(seed), 8)
    return {
        "hidden_states": draw_hidden_states(jax.random.fold_in(splits[7], 71), 0),
        "w_query": draw_w_query(jax.random.fold_in(splits[7], 71), 0),
        "w_key_value": draw_w_key_value(jax.random.fold_in(splits[7], 71), 0),
        "adapter_down": bell_draw(splits[3], (ADAPTERS, D, RANK), D ** -0.5, 0.15625, ((0, 16), (1, 4))),
        "adapter_up": bell_draw(splits[4], (ADAPTERS, RANK, HEADS * HEAD_DIM), RANK ** -0.5, 1.5, ((0, 16), (2, 4))),
        "req_lengths": jax.vmap(lambda own: uneven(own, REQ_DEV, GROUP_TOK - PREFIX, MOST_LEN, 1))(jax.random.split(splits[5], N_DP)).reshape((N_DP, REQ_DEV)).astype(jnp.int32),
        "req_adapter": draw_req_adapter(jax.random.fold_in(splits[7], 71), 0),
    }


masked_score = -1e+30

def one_block(hidden, lengths_row, adapters_row, w_query, w_key_value, adapter_down, adapter_up):
    block_len = hidden.shape[0]
    requests = lengths_row.shape[0]
    prefix_len = (block_len - jnp.sum(lengths_row)).astype(jnp.int32)
    ends_at = (jnp.cumsum(lengths_row) + prefix_len).astype(jnp.int32)
    starts = (ends_at - lengths_row).astype(jnp.int32)
    positions = jnp.arange(block_len, dtype=jnp.int32)
    segment = lax.optimization_barrier(jnp.sum((positions[:, None] >= starts[None, :]).astype(jnp.int32), axis=1)).astype(jnp.int32)
    chosen_down = jnp.transpose(adapter_down[adapters_row], (1, 0, 2)).reshape(D, requests * RANK)
    chosen_up = adapter_up[adapters_row].reshape(requests * RANK, HEADS * HEAD_DIM).astype(jnp.float32)
    reduced = jnp.dot(hidden, chosen_down, preferred_element_type=jnp.float32)
    kept_cols = (jnp.arange(requests * RANK, dtype=jnp.int32) // RANK)[None, :] == (segment - 1)[:, None]
    reduced = jnp.where(kept_cols, reduced, jnp.float32(0.0))
    adapter_term = jnp.dot(reduced, chosen_up, precision=lax.Precision.HIGHEST)
    query_rows = (jnp.dot(hidden, w_query, preferred_element_type=jnp.float32) + adapter_term).astype(jnp.bfloat16)
    kv_cache = jnp.dot(hidden, w_key_value, preferred_element_type=jnp.float32).astype(jnp.bfloat16)
    allowed = (positions[None, :] <= positions[:, None]) & ((segment[None, :] == segment[:, None]) | (segment[None, :] == 0))
    per_group = HEADS // KV_HEADS
    kv_width = KV_HEADS * HEAD_DIM
    score_scale = 1.0 / math.sqrt(HEAD_DIM)

    def one_head(head_index):
        kv_group = head_index // per_group
        query_head = lax.dynamic_slice_in_dim(query_rows, head_index * HEAD_DIM, HEAD_DIM, 1)
        key_head = lax.dynamic_slice_in_dim(kv_cache, kv_group * HEAD_DIM, HEAD_DIM, 1)
        value_head = lax.dynamic_slice_in_dim(kv_cache, kv_width + kv_group * HEAD_DIM, HEAD_DIM, 1)
        scores = jnp.dot(query_head, key_head.T, preferred_element_type=jnp.float32) * score_scale
        scores = jnp.where(allowed, scores, masked_score)
        row_max = lax.optimization_barrier(jnp.max(scores, axis=1, keepdims=True))
        exponent = jnp.where(allowed, jnp.exp(scores - row_max), jnp.float32(0.0))
        row_sum = lax.optimization_barrier(jnp.sum(exponent, axis=1, keepdims=True))
        head_out = jnp.dot(exponent.astype(jnp.bfloat16), value_head, preferred_element_type=jnp.float32) / row_sum
        return head_out.astype(jnp.bfloat16)
    heads_out = lax.map(one_head, jnp.arange(HEADS, dtype=jnp.int32))
    attention = jnp.transpose(heads_out, (1, 0, 2)).reshape(block_len, HEADS * HEAD_DIM)
    return (attention, kv_cache)

def reference(hidden_states, w_query, w_key_value, adapter_down, adapter_up, req_lengths, req_adapter):
    blocks = hidden_states.reshape(N_DP, GROUP_TOK, D)

    def run_block(block_items):
        return one_block(block_items[0], block_items[1], block_items[2], w_query, w_key_value, adapter_down, adapter_up)
    attention, kv_cache = lax.map(run_block, (blocks, req_lengths, req_adapter))
    return (attention.reshape(TOKENS, HEADS * HEAD_DIM), kv_cache.reshape(TOKENS, 2 * KV_HEADS * HEAD_DIM))
```

```python
import math

import jax
import jax.numpy as jnp
from jax import lax
from jax.sharding import PartitionSpec as P

HEAD_DIM = 128
MOST_LEN = 160


masked_score = -1e30


def block_layout(lengths_row, block_len):
    prefix_len = block_len - jnp.sum(lengths_row)
    ends_at = jnp.cumsum(lengths_row) + prefix_len
    starts = ends_at - lengths_row
    positions = jnp.arange(block_len, dtype=jnp.int32)
    segment = jnp.sum((positions[:, None] >= starts[None, :]).astype(jnp.int32), axis=1)
    return (starts, segment, positions)


def slot_numbers(holders):
    request_total = holders.shape[0]
    ordering = jnp.arange(request_total, dtype=jnp.int32)
    earlier = ordering[None, :] < ordering[:, None]
    same_holder = holders[:, None] == holders[None, :]
    return jnp.sum((earlier & same_holder).astype(jnp.int32), axis=1)


def make_attend(query_rows, segment, first_row, kv_group, head_size, kv_half):
    own_rows = query_rows.shape[0]
    heads_here = query_rows.shape[1] // head_size
    query_heads = query_rows.reshape(own_rows, heads_here, head_size)
    query_pos = first_row + jnp.arange(own_rows, dtype=jnp.int32)
    query_seg = lax.dynamic_slice_in_dim(segment, first_row, own_rows, 0)
    score_scale = 1.0 / math.sqrt(head_size)

    def attend(state_in, key_block, key_start):
        running_max, running_sum, running_out = state_in
        block_size = key_block.shape[0]
        key_rows = lax.dynamic_slice_in_dim(key_block, kv_group * head_size, head_size, 1)
        values = lax.dynamic_slice_in_dim(key_block, kv_half + kv_group * head_size, head_size, 1)
        key_pos = jnp.arange(block_size, dtype=jnp.int32)
        allowed = (key_pos[None, :] <= query_pos[:, None]) & (
            (segment[None, :] == query_seg[:, None]) | (segment[None, :] == 0)
        )
        scores = (
            jnp.einsum("qhd,kd->hqk", query_heads, key_rows, preferred_element_type=jnp.float32)
            * score_scale
        )
        scores = jnp.where(allowed[None], scores, masked_score)
        new_max = jnp.maximum(running_max, jnp.max(scores, axis=2))
        weights = jnp.where(allowed[None], jnp.exp(scores - new_max[:, :, None]), 0.0)
        running_sum = jnp.sum(weights, axis=2)
        running_out = jnp.einsum(
            "hqk,kd->hqd", weights.astype(jnp.bfloat16), values, preferred_element_type=jnp.float32
        )
        return (new_max, running_sum, running_out)

    initial = (
        jnp.full((heads_here, own_rows), masked_score, jnp.float32),
        jnp.zeros((heads_here, own_rows), jnp.float32),
        jnp.zeros((heads_here, own_rows, head_size), jnp.float32),
    )
    return (attend, initial)


def body(hidden_states, w_query, w_key_value, adapter_down, adapter_up, req_lengths, req_adapter):
    dp_size = lax.axis_size("dp")
    block_index = lax.axis_index("dp")
    col_index = lax.axis_index("col")
    row_index = lax.axis_index("row")
    gathered = lax.all_gather(hidden_states, "row", axis=0, tiled=True)
    block_len = gathered.shape[0]
    query_cols = w_query.shape[1]
    kv_cols = w_key_value.shape[1]
    kv_half = kv_cols // 2
    head_size = HEAD_DIM
    heads_here = query_cols // head_size
    heads_total = heads_here * lax.axis_size("row")
    kv_heads = kv_half // head_size
    kv_group = row_index * heads_here // (heads_total // kv_heads)
    own_rows = block_len // lax.axis_size("col")
    first_row = col_index * own_rows
    held_sets = adapter_down.shape[0]
    width_here = adapter_down.shape[1]
    rank_size = adapter_down.shape[2]
    lengths_row = req_lengths[block_index]
    adapters_row = req_adapter[block_index]
    requests = lengths_row.shape[0]
    starts, segment, positions = block_layout(lengths_row, block_len)
    request_of = jnp.clip(segment - 1, 0, requests - 1)
    in_request = segment > 0
    holders = adapters_row // held_sets
    wanted_from_me = (req_adapter // held_sets) == block_index
    local_pick = jnp.sum(jnp.where(wanted_from_me, req_adapter % held_sets, 0), axis=1)
    down_pick = jnp.transpose(jnp.take(adapter_down, local_pick, axis=0), (0, 2, 1))
    up_pick = jnp.take(adapter_up, local_pick, axis=0)
    outgoing = jnp.concatenate([down_pick, up_pick], axis=1)
    incoming = lax.all_to_all(outgoing, "dp", split_axis=0, concat_axis=0, tiled=True)
    flat_down = incoming[:, :rank_size, :].reshape(dp_size * rank_size, width_here).T
    flat_up = incoming[:, rank_size:, :].reshape(dp_size * rank_size, query_cols).astype(jnp.float32)
    rank_owner = jnp.arange(dp_size * rank_size, dtype=jnp.int32) // rank_size
    reduced = jnp.dot(gathered, flat_down, preferred_element_type=jnp.float32)
    token_holder = jnp.where(in_request, holders[request_of], -1)
    kept_cols = rank_owner[None, :] == token_holder[:, None]
    reduced = jnp.where(kept_cols, reduced, 0.0)
    adapter_term = jnp.dot(reduced, flat_up, precision=lax.Precision.HIGHEST)
    both_weights = jnp.concatenate([w_query, w_key_value], axis=1)
    partial_value = jnp.dot(gathered, both_weights, preferred_element_type=jnp.float32)
    summed = lax.psum_scatter(
        partial_value
        + jnp.concatenate(
            [adapter_term, jnp.zeros((own_rows * lax.axis_size("col"), kv_cols), jnp.float32)],
            axis=1,
        ),
        "col",
        scatter_dimension=0,
        tiled=True,
    )
    query_rows = summed[:, :query_cols].astype(jnp.bfloat16)
    kv_cache = summed[:, query_cols:].astype(jnp.bfloat16)
    attend, initial = make_attend(query_rows, segment, first_row, kv_group, head_size, kv_half)
    running_max, running_sum, running_out = attend(
        initial, lax.all_gather(kv_cache, "col", axis=0, tiled=True), jnp.int32(0)
    )
    attention = (running_out / running_sum[:, :, None]).astype(jnp.bfloat16)
    attention = jnp.transpose(attention, (1, 0, 2)).reshape(own_rows, query_cols)
    return (attention, kv_cache)


def solution(mesh):
    return jax.shard_map(
        body,
        mesh=mesh,
        in_specs=(
            P(("dp", "row"), "col"),
            P("col", "row"),
            P("col", None),
            P("dp", "col", None),
            P("dp", None, "row"),
            P(),
            P(),
        ),
        out_specs=(P(("dp", "col"), "row"), P(("dp", "col"), None)),
        check_vma=False,
    )
```

```python
import math

import jax
import jax.numpy as jnp
from jax import lax
from jax.sharding import PartitionSpec as P

HEAD_DIM = 128
MOST_LEN = 160


masked_score = -1e30


def block_layout(lengths_row, block_len):
    prefix_len = block_len - jnp.sum(lengths_row)
    ends_at = jnp.cumsum(lengths_row) + prefix_len
    starts = ends_at - lengths_row
    positions = jnp.arange(block_len, dtype=jnp.int32)
    segment = jnp.sum((positions[:, None] >= starts[None, :]).astype(jnp.int32), axis=1)
    return (starts, segment, positions)


def slot_numbers(holders):
    request_total = holders.shape[0]
    ordering = jnp.arange(request_total, dtype=jnp.int32)
    earlier = ordering[None, :] < ordering[:, None]
    same_holder = holders[:, None] == holders[None, :]
    return jnp.sum((earlier & same_holder).astype(jnp.int32), axis=1)


def make_attend(query_rows, segment, first_row, kv_group, head_size, kv_half):
    own_rows = query_rows.shape[0]
    heads_here = query_rows.shape[1] // head_size
    query_heads = query_rows.reshape(own_rows, heads_here, head_size)
    query_pos = first_row + jnp.arange(own_rows, dtype=jnp.int32)
    query_seg = lax.dynamic_slice_in_dim(segment, first_row, own_rows, 0)
    score_scale = 1.0 / math.sqrt(head_size)

    def attend(state_in, key_block, key_start):
        running_max, running_sum, running_out = state_in
        block_size = key_block.shape[0]
        key_rows = lax.dynamic_slice_in_dim(key_block, kv_group * head_size, head_size, 1)
        values = lax.dynamic_slice_in_dim(key_block, kv_half + kv_group * head_size, head_size, 1)
        key_pos = jnp.arange(block_size, dtype=jnp.int32)
        allowed = (key_pos[None, :] <= query_pos[:, None]) & (
            (segment[None, :] == query_seg[:, None]) | (segment[None, :] == 0)
        )
        scores = (
            jnp.einsum("qhd,kd->hqk", query_heads, key_rows, preferred_element_type=jnp.float32)
            * score_scale
        )
        scores = jnp.where(allowed[None], scores, masked_score)
        new_max = jnp.maximum(running_max, jnp.max(scores, axis=2))
        weights = jnp.where(allowed[None], jnp.exp(scores - new_max[:, :, None]), 0.0)
        running_sum = jnp.sum(weights, axis=2)
        running_out = jnp.einsum(
            "hqk,kd->hqd", weights.astype(jnp.bfloat16), values, preferred_element_type=jnp.float32
        )
        return (new_max, running_sum, running_out)

    initial = (
        jnp.full((heads_here, own_rows), masked_score, jnp.float32),
        jnp.zeros((heads_here, own_rows), jnp.float32),
        jnp.zeros((heads_here, own_rows, head_size), jnp.float32),
    )
    return (attend, initial)


def body(hidden_states, w_query, w_key_value, adapter_down, adapter_up, req_lengths, req_adapter):
    dp_size = lax.axis_size("dp")
    block_index = lax.axis_index("dp")
    col_index = lax.axis_index("col")
    row_index = lax.axis_index("row")
    gathered = lax.all_gather(hidden_states, "row", axis=0, tiled=True)
    block_len = gathered.shape[0]
    query_cols = w_query.shape[1]
    kv_cols = w_key_value.shape[1]
    kv_half = kv_cols // 2
    head_size = HEAD_DIM
    heads_here = query_cols // head_size
    heads_total = heads_here * lax.axis_size("row")
    kv_heads = kv_half // head_size
    kv_group = row_index * heads_here // (heads_total // kv_heads)
    own_rows = block_len // lax.axis_size("col")
    first_row = col_index * own_rows
    held_sets = adapter_down.shape[0]
    width_here = adapter_down.shape[1]
    rank_size = adapter_down.shape[2]
    lengths_row = req_lengths[block_index]
    adapters_row = req_adapter[block_index]
    requests = lengths_row.shape[0]
    starts, segment, positions = block_layout(lengths_row, block_len)
    request_of = jnp.clip(segment - 1, 0, requests - 1)
    in_request = segment > 0
    holders = adapters_row // held_sets
    wanted_from_me = (req_adapter // held_sets) == block_index
    local_pick = jnp.sum(jnp.where(wanted_from_me, req_adapter % held_sets, 0), axis=1)
    down_pick = jnp.transpose(jnp.take(adapter_down, local_pick, axis=0), (0, 2, 1))
    up_pick = jnp.take(adapter_up, local_pick, axis=0)
    outgoing = jnp.concatenate([down_pick, up_pick], axis=1)
    incoming = lax.all_to_all(outgoing, "dp", split_axis=0, concat_axis=0, tiled=True)
    flat_down = incoming[:, :rank_size, :].reshape(dp_size * rank_size, width_here).T
    flat_up = incoming[:, rank_size:, :].reshape(dp_size * rank_size, query_cols).astype(jnp.float32)
    rank_owner = jnp.arange(dp_size * rank_size, dtype=jnp.int32) // rank_size
    reduced = jnp.dot(gathered, flat_down, preferred_element_type=jnp.float32)
    token_holder = jnp.where(in_request, holders[request_of], -1)
    kept_cols = rank_owner[None, :] == token_holder[:, None]
    reduced = jnp.where(kept_cols, reduced, 0.0)
    adapter_term = jnp.dot(reduced, flat_up, precision=lax.Precision.HIGHEST)
    kv_share = kv_cols // lax.axis_size("row")
    kv_slice = lax.dynamic_slice_in_dim(w_key_value, row_index * kv_share, kv_share, 1)
    both_weights = jnp.concatenate([w_query, kv_slice], axis=1)
    partial_value = jnp.dot(gathered, both_weights, preferred_element_type=jnp.float32)
    summed = lax.psum_scatter(
        partial_value
        + jnp.concatenate(
            [adapter_term, jnp.zeros((own_rows * lax.axis_size("col"), kv_share), jnp.float32)],
            axis=1,
        ),
        "col",
        scatter_dimension=0,
        tiled=True,
    )
    query_rows = summed[:, :query_cols].astype(jnp.bfloat16)
    kv_cache = lax.all_gather(summed[:, query_cols:].astype(jnp.bfloat16), "row", axis=1, tiled=True)
    head_kv = jnp.concatenate(
        [
            lax.dynamic_slice_in_dim(kv_cache, kv_group * head_size, head_size, 1),
            lax.dynamic_slice_in_dim(kv_cache, kv_half + kv_group * head_size, head_size, 1),
        ],
        axis=1,
    )
    attend, initial = make_attend(query_rows, segment, first_row, 0, head_size, head_size)
    running_max, running_sum, running_out = attend(
        initial, lax.all_gather(head_kv, "col", axis=0, tiled=True), jnp.int32(0)
    )
    attention = (running_out / running_sum[:, :, None]).astype(jnp.bfloat16)
    attention = jnp.transpose(attention, (1, 0, 2)).reshape(own_rows, query_cols)
    return (attention, kv_cache)


def solution(mesh):
    return jax.shard_map(
        body,
        mesh=mesh,
        in_specs=(
            P(("dp", "row"), "col"),
            P("col", "row"),
            P("col", None),
            P("dp", "col", None),
            P("dp", None, "row"),
            P(),
            P(),
        ),
        out_specs=(P(("dp", "col"), "row"), P(("dp", "col"), None)),
        check_vma=False,
    )
```

```python
import math

import jax
import jax.numpy as jnp
from jax import lax
from jax.sharding import PartitionSpec as P

HEAD_DIM = 128
MOST_LEN = 160


masked_score = -1e30


def block_layout(lengths_row, block_len):
    prefix_len = block_len - jnp.sum(lengths_row)
    ends_at = jnp.cumsum(lengths_row) + prefix_len
    starts = ends_at - lengths_row
    positions = jnp.arange(block_len, dtype=jnp.int32)
    segment = jnp.sum((positions[:, None] >= starts[None, :]).astype(jnp.int32), axis=1)
    return (starts, segment, positions)


def slot_numbers(holders):
    request_total = holders.shape[0]
    ordering = jnp.arange(request_total, dtype=jnp.int32)
    earlier = ordering[None, :] < ordering[:, None]
    same_holder = holders[:, None] == holders[None, :]
    return jnp.sum((earlier & same_holder).astype(jnp.int32), axis=1)


def make_attend(query_rows, segment, first_row, kv_group, head_size, kv_half):
    own_rows = query_rows.shape[0]
    heads_here = query_rows.shape[1] // head_size
    query_heads = query_rows.reshape(own_rows, heads_here, head_size)
    query_pos = first_row + jnp.arange(own_rows, dtype=jnp.int32)
    query_seg = lax.dynamic_slice_in_dim(segment, first_row, own_rows, 0)
    score_scale = 1.0 / math.sqrt(head_size)

    def attend(state_in, key_block, key_start):
        running_max, running_sum, running_out = state_in
        block_size = key_block.shape[0]
        key_rows = lax.dynamic_slice_in_dim(key_block, kv_group * head_size, head_size, 1)
        values = lax.dynamic_slice_in_dim(key_block, kv_half + kv_group * head_size, head_size, 1)
        key_pos = jnp.arange(block_size, dtype=jnp.int32)
        allowed = (key_pos[None, :] <= query_pos[:, None]) & (
            (segment[None, :] == query_seg[:, None]) | (segment[None, :] == 0)
        )
        scores = (
            jnp.einsum("qhd,kd->hqk", query_heads, key_rows, preferred_element_type=jnp.float32)
            * score_scale
        )
        scores = jnp.where(allowed[None], scores, masked_score)
        new_max = jnp.maximum(running_max, jnp.max(scores, axis=2))
        weights = jnp.where(allowed[None], jnp.exp(scores - new_max[:, :, None]), 0.0)
        running_sum = jnp.sum(weights, axis=2)
        running_out = jnp.einsum(
            "hqk,kd->hqd", weights.astype(jnp.bfloat16), values, preferred_element_type=jnp.float32
        )
        return (new_max, running_sum, running_out)

    initial = (
        jnp.full((heads_here, own_rows), masked_score, jnp.float32),
        jnp.zeros((heads_here, own_rows), jnp.float32),
        jnp.zeros((heads_here, own_rows, head_size), jnp.float32),
    )
    return (attend, initial)


def body(hidden_states, w_query, w_key_value, adapter_down, adapter_up, req_lengths, req_adapter):
    dp_size = lax.axis_size("dp")
    block_index = lax.axis_index("dp")
    col_index = lax.axis_index("col")
    row_index = lax.axis_index("row")
    gathered = lax.all_gather(hidden_states, "row", axis=0, tiled=True)
    block_len = gathered.shape[0]
    query_cols = w_query.shape[1]
    kv_cols = w_key_value.shape[1]
    kv_half = kv_cols // 2
    head_size = HEAD_DIM
    heads_here = query_cols // head_size
    heads_total = heads_here * lax.axis_size("row")
    kv_heads = kv_half // head_size
    kv_group = row_index * heads_here // (heads_total // kv_heads)
    own_rows = block_len // lax.axis_size("col")
    first_row = col_index * own_rows
    held_sets = adapter_down.shape[0]
    width_here = adapter_down.shape[1]
    rank_size = adapter_down.shape[2]
    lengths_row = req_lengths[block_index]
    adapters_row = req_adapter[block_index]
    requests = lengths_row.shape[0]
    starts, segment, positions = block_layout(lengths_row, block_len)
    request_of = jnp.clip(segment - 1, 0, requests - 1)
    in_request = segment > 0
    holders = adapters_row // held_sets
    wanted_from_me = (req_adapter // held_sets) == block_index
    local_pick = jnp.sum(jnp.where(wanted_from_me, req_adapter % held_sets, 0), axis=1)
    down_pick = jnp.transpose(jnp.take(adapter_down, local_pick, axis=0), (0, 2, 1))
    up_pick = jnp.take(adapter_up, local_pick, axis=0)
    outgoing = jnp.concatenate([down_pick, up_pick], axis=1)
    incoming = lax.all_to_all(outgoing, "dp", split_axis=0, concat_axis=0, tiled=True)
    flat_down = incoming[:, :rank_size, :].reshape(dp_size * rank_size, width_here).T
    flat_up = incoming[:, rank_size:, :].reshape(dp_size * rank_size, query_cols).astype(jnp.float32)
    rank_owner = jnp.arange(dp_size * rank_size, dtype=jnp.int32) // rank_size
    reduced = jnp.dot(gathered, flat_down, preferred_element_type=jnp.float32)
    request_ids = jnp.arange(requests, dtype=jnp.int32)
    token_holder = jnp.sum(
        jnp.where(segment[:, None] == request_ids[None, :] + 1, holders[None, :] + 1, 0), axis=1
    ) - 1
    kept_cols = rank_owner[None, :] == token_holder[:, None]
    reduced = jnp.where(kept_cols, reduced, 0.0)
    adapter_term = jnp.dot(reduced, flat_up, precision=lax.Precision.HIGHEST)
    kv_share = kv_cols // lax.axis_size("row")
    kv_slice = lax.dynamic_slice_in_dim(w_key_value, row_index * kv_share, kv_share, 1)
    both_weights = jnp.concatenate([w_query, kv_slice], axis=1)
    partial_value = jnp.dot(gathered, both_weights, preferred_element_type=jnp.float32)
    summed = lax.psum_scatter(
        partial_value
        + jnp.concatenate(
            [adapter_term, jnp.zeros((own_rows * lax.axis_size("col"), kv_share), jnp.float32)],
            axis=1,
        ),
        "col",
        scatter_dimension=0,
        tiled=True,
    )
    query_rows = summed[:, :query_cols].astype(jnp.bfloat16)
    kv_pieces = lax.all_gather(summed[:, query_cols:].astype(jnp.bfloat16), ("row", "col"), axis=0)
    kv_pieces = kv_pieces.reshape(lax.axis_size("row"), lax.axis_size("col"), own_rows, kv_share)
    own_pieces = lax.dynamic_index_in_dim(kv_pieces, col_index, 1, keepdims=False)
    kv_cache = jnp.transpose(own_pieces, (1, 0, 2)).reshape(own_rows, kv_cols)
    parts_per_head = head_size // kv_share
    key_all = lax.dynamic_slice_in_dim(kv_pieces, kv_group * parts_per_head, parts_per_head, 0)
    value_all = lax.dynamic_slice_in_dim(
        kv_pieces, (kv_heads + kv_group) * parts_per_head, parts_per_head, 0
    )
    key_all = jnp.transpose(key_all, (1, 2, 0, 3)).reshape(block_len, head_size)
    value_all = jnp.transpose(value_all, (1, 2, 0, 3)).reshape(block_len, head_size)
    attend, initial = make_attend(query_rows, segment, first_row, 0, head_size, head_size)
    running_max, running_sum, running_out = attend(
        initial, jnp.concatenate([key_all, value_all], axis=1), jnp.int32(0)
    )
    attention = (running_out / running_sum[:, :, None]).astype(jnp.bfloat16)
    attention = jnp.transpose(attention, (1, 0, 2)).reshape(own_rows, query_cols)
    return (attention, kv_cache)


def solution(mesh):
    return jax.shard_map(
        body,
        mesh=mesh,
        in_specs=(
            P(("dp", "row"), "col"),
            P("col", "row"),
            P("col", None),
            P("dp", "col", None),
            P("dp", None, "row"),
            P(),
            P(),
        ),
        out_specs=(P(("dp", "col"), "row"), P(("dp", "col"), None)),
        check_vma=False,
    )
```

```python
import math

import jax
import jax.numpy as jnp
from jax import lax
from jax.sharding import PartitionSpec as P

HEAD_DIM = 128
MOST_LEN = 160


masked_score = -1e30


def block_layout(lengths_row, block_len):
    prefix_len = block_len - jnp.sum(lengths_row)
    ends_at = jnp.cumsum(lengths_row) + prefix_len
    starts = ends_at - lengths_row
    positions = jnp.arange(block_len, dtype=jnp.int32)
    segment = jnp.sum((positions[:, None] >= starts[None, :]).astype(jnp.int32), axis=1)
    return (starts, segment, positions)


def slot_numbers(holders):
    request_total = holders.shape[0]
    ordering = jnp.arange(request_total, dtype=jnp.int32)
    earlier = ordering[None, :] < ordering[:, None]
    same_holder = holders[:, None] == holders[None, :]
    return jnp.sum((earlier & same_holder).astype(jnp.int32), axis=1)


def make_attend(query_rows, segment, first_row, kv_group, head_size, kv_half):
    own_rows = query_rows.shape[0]
    heads_here = query_rows.shape[1] // head_size
    query_heads = query_rows.reshape(own_rows, heads_here, head_size)
    query_pos = first_row + jnp.arange(own_rows, dtype=jnp.int32)
    query_seg = lax.dynamic_slice_in_dim(segment, first_row, own_rows, 0)
    score_scale = 1.0 / math.sqrt(head_size)

    def attend(state_in, key_block, key_start):
        running_max, running_sum, running_out = state_in
        block_size = key_block.shape[0]
        key_rows = lax.dynamic_slice_in_dim(key_block, kv_group * head_size, head_size, 1)
        values = lax.dynamic_slice_in_dim(key_block, kv_half + kv_group * head_size, head_size, 1)
        key_pos = jnp.arange(block_size, dtype=jnp.int32)
        allowed = (key_pos[None, :] <= query_pos[:, None]) & (
            (segment[None, :] == query_seg[:, None]) | (segment[None, :] == 0)
        )
        scores = (
            jnp.einsum("qhd,kd->hqk", query_heads, key_rows, preferred_element_type=jnp.float32)
            * score_scale
        )
        scores = jnp.where(allowed[None], scores, masked_score)
        new_max = jnp.maximum(running_max, jnp.max(scores, axis=2))
        weights = jnp.where(allowed[None], jnp.exp(scores - new_max[:, :, None]), 0.0)
        running_sum = jnp.sum(weights, axis=2)
        running_out = jnp.einsum(
            "hqk,kd->hqd", weights.astype(jnp.bfloat16), values, preferred_element_type=jnp.float32
        )
        return (new_max, running_sum, running_out)

    initial = (
        jnp.full((heads_here, own_rows), masked_score, jnp.float32),
        jnp.zeros((heads_here, own_rows), jnp.float32),
        jnp.zeros((heads_here, own_rows, head_size), jnp.float32),
    )
    return (attend, initial)


def shifted_copies(x, axis_name):
    size = lax.axis_size(axis_name)
    copies = [x]
    for shift in range(1, size):
        perm = [(i, (i - shift) % size) for i in range(size)]
        copies.append(lax.ppermute(x, axis_name, perm))
    return copies


def ring_gather(x, axis_name, axis):
    size = lax.axis_size(axis_name)
    me = lax.axis_index(axis_name)
    copies = shifted_copies(x, axis_name)
    doubled = jnp.stack(copies + copies, axis=0)
    ordered = lax.dynamic_slice_in_dim(doubled, size - me, size, 0)
    moved = jnp.moveaxis(ordered, 0, axis)
    shape = list(x.shape)
    shape[axis] = shape[axis] * size
    return moved.reshape(shape)


def ring_reduce_scatter(x, axis_name):
    size = lax.axis_size(axis_name)
    me = lax.axis_index(axis_name)
    chunk = x.shape[0] // size
    total = lax.dynamic_slice_in_dim(x, me * chunk, chunk, 0)
    for shift in range(1, size):
        perm = [(i, (i + shift) % size) for i in range(size)]
        piece = lax.dynamic_slice_in_dim(x, ((me + shift) % size) * chunk, chunk, 0)
        total = total + lax.ppermute(piece, axis_name, perm)
    return total


def body(hidden_states, w_query, w_key_value, adapter_down, adapter_up, req_lengths, req_adapter):
    dp_size = lax.axis_size("dp")
    block_index = lax.axis_index("dp")
    col_index = lax.axis_index("col")
    row_index = lax.axis_index("row")
    gathered = ring_gather(hidden_states, "row", 0)
    block_len = gathered.shape[0]
    query_cols = w_query.shape[1]
    kv_cols = w_key_value.shape[1]
    kv_half = kv_cols // 2
    head_size = HEAD_DIM
    heads_here = query_cols // head_size
    heads_total = heads_here * lax.axis_size("row")
    kv_heads = kv_half // head_size
    kv_group = row_index * heads_here // (heads_total // kv_heads)
    own_rows = block_len // lax.axis_size("col")
    first_row = col_index * own_rows
    held_sets = adapter_down.shape[0]
    width_here = adapter_down.shape[1]
    rank_size = adapter_down.shape[2]
    lengths_row = req_lengths[block_index]
    adapters_row = req_adapter[block_index]
    requests = lengths_row.shape[0]
    starts, segment, positions = block_layout(lengths_row, block_len)
    request_of = jnp.clip(segment - 1, 0, requests - 1)
    in_request = segment > 0
    holders = adapters_row // held_sets
    wanted_from_me = (req_adapter // held_sets) == block_index
    local_pick = jnp.sum(jnp.where(wanted_from_me, req_adapter % held_sets, 0), axis=1)
    down_pick = jnp.transpose(jnp.take(adapter_down, local_pick, axis=0), (0, 2, 1))
    up_pick = jnp.take(adapter_up, local_pick, axis=0)
    outgoing = jnp.concatenate([down_pick, up_pick], axis=1)
    incoming = lax.all_to_all(outgoing, "dp", split_axis=0, concat_axis=0, tiled=True)
    flat_down = incoming[:, :rank_size, :].reshape(dp_size * rank_size, width_here).T
    flat_up = incoming[:, rank_size:, :].reshape(dp_size * rank_size, query_cols).astype(jnp.float32)
    rank_owner = jnp.arange(dp_size * rank_size, dtype=jnp.int32) // rank_size
    reduced = jnp.dot(gathered, flat_down, preferred_element_type=jnp.float32)
    request_ids = jnp.arange(requests, dtype=jnp.int32)
    token_holder = jnp.sum(
        jnp.where(segment[:, None] == request_ids[None, :] + 1, holders[None, :] + 1, 0), axis=1
    ) - 1
    kept_cols = rank_owner[None, :] == token_holder[:, None]
    reduced = jnp.where(kept_cols, reduced, 0.0)
    adapter_term = jnp.dot(reduced, flat_up, precision=lax.Precision.HIGHEST)
    kv_share = kv_cols // lax.axis_size("row")
    kv_slice = lax.dynamic_slice_in_dim(w_key_value, row_index * kv_share, kv_share, 1)
    both_weights = jnp.concatenate([w_query, kv_slice], axis=1)
    partial_value = jnp.dot(gathered, both_weights, preferred_element_type=jnp.float32)
    summed = ring_reduce_scatter(
        partial_value
        + jnp.concatenate(
            [adapter_term, jnp.zeros((own_rows * lax.axis_size("col"), kv_share), jnp.float32)],
            axis=1,
        ),
        "col",
    )
    query_rows = summed[:, :query_cols].astype(jnp.bfloat16)
    kv_cache = ring_gather(summed[:, query_cols:].astype(jnp.bfloat16), "row", 1)
    head_kv = jnp.concatenate(
        [
            lax.dynamic_slice_in_dim(kv_cache, kv_group * head_size, head_size, 1),
            lax.dynamic_slice_in_dim(kv_cache, kv_half + kv_group * head_size, head_size, 1),
        ],
        axis=1,
    )
    attend, initial = make_attend(query_rows, segment, first_row, 0, head_size, head_size)
    running_max, running_sum, running_out = attend(
        initial, ring_gather(head_kv, "col", 0), jnp.int32(0)
    )
    attention = (running_out / running_sum[:, :, None]).astype(jnp.bfloat16)
    attention = jnp.transpose(attention, (1, 0, 2)).reshape(own_rows, query_cols)
    return (attention, kv_cache)


def solution(mesh):
    return jax.shard_map(
        body,
        mesh=mesh,
        in_specs=(
            P(("dp", "row"), "col"),
            P("col", "row"),
            P("col", None),
            P("dp", "col", None),
            P("dp", None, "row"),
            P(),
            P(),
        ),
        out_specs=(P(("dp", "col"), "row"), P(("dp", "col"), None)),
        check_vma=False,
    )
```

```python
import math

import jax
import jax.numpy as jnp
from jax import lax
from jax.sharding import PartitionSpec as P

HEAD_DIM = 128
MOST_LEN = 160


masked_score = -1e30


def block_layout(lengths_row, block_len):
    prefix_len = block_len - jnp.sum(lengths_row)
    ends_at = jnp.cumsum(lengths_row) + prefix_len
    starts = ends_at - lengths_row
    positions = jnp.arange(block_len, dtype=jnp.int32)
    segment = jnp.sum((positions[:, None] >= starts[None, :]).astype(jnp.int32), axis=1)
    return (starts, segment, positions)


def slot_numbers(holders):
    request_total = holders.shape[0]
    ordering = jnp.arange(request_total, dtype=jnp.int32)
    earlier = ordering[None, :] < ordering[:, None]
    same_holder = holders[:, None] == holders[None, :]
    return jnp.sum((earlier & same_holder).astype(jnp.int32), axis=1)


def make_attend(query_rows, segment, first_row, kv_group, head_size, kv_half):
    own_rows = query_rows.shape[0]
    heads_here = query_rows.shape[1] // head_size
    query_heads = query_rows.reshape(own_rows, heads_here, head_size)
    query_pos = first_row + jnp.arange(own_rows, dtype=jnp.int32)
    query_seg = lax.dynamic_slice_in_dim(segment, first_row, own_rows, 0)
    score_scale = 1.0 / math.sqrt(head_size)

    def attend(state_in, key_block, key_start):
        running_max, running_sum, running_out = state_in
        block_size = key_block.shape[0]
        key_rows = lax.dynamic_slice_in_dim(key_block, kv_group * head_size, head_size, 1)
        values = lax.dynamic_slice_in_dim(key_block, kv_half + kv_group * head_size, head_size, 1)
        key_pos = jnp.arange(block_size, dtype=jnp.int32)
        allowed = (key_pos[None, :] <= query_pos[:, None]) & (
            (segment[None, :] == query_seg[:, None]) | (segment[None, :] == 0)
        )
        scores = (
            jnp.einsum("qhd,kd->hqk", query_heads, key_rows, preferred_element_type=jnp.float32)
            * score_scale
        )
        scores = jnp.where(allowed[None], scores, masked_score)
        new_max = jnp.maximum(running_max, jnp.max(scores, axis=2))
        weights = jnp.where(allowed[None], jnp.exp(scores - new_max[:, :, None]), 0.0)
        running_sum = jnp.sum(weights, axis=2)
        running_out = jnp.einsum(
            "hqk,kd->hqd", weights.astype(jnp.bfloat16), values, preferred_element_type=jnp.float32
        )
        return (new_max, running_sum, running_out)

    initial = (
        jnp.full((heads_here, own_rows), masked_score, jnp.float32),
        jnp.zeros((heads_here, own_rows), jnp.float32),
        jnp.zeros((heads_here, own_rows, head_size), jnp.float32),
    )
    return (attend, initial)


def shifted_copies(x, axis_name):
    size = lax.axis_size(axis_name)
    copies = [x]
    for shift in range(1, size):
        perm = [(i, (i - shift) % size) for i in range(size)]
        copies.append(lax.ppermute(x, axis_name, perm))
    return copies


def ring_gather(x, axis_name, axis):
    size = lax.axis_size(axis_name)
    me = lax.axis_index(axis_name)
    copies = shifted_copies(x, axis_name)
    doubled = jnp.stack(copies + copies, axis=0)
    ordered = lax.dynamic_slice_in_dim(doubled, size - me, size, 0)
    moved = jnp.moveaxis(ordered, 0, axis)
    shape = list(x.shape)
    shape[axis] = shape[axis] * size
    return moved.reshape(shape)


def ring_reduce_scatter(x, axis_name):
    size = lax.axis_size(axis_name)
    me = lax.axis_index(axis_name)
    chunk = x.shape[0] // size
    total = lax.dynamic_slice_in_dim(x, me * chunk, chunk, 0)
    for shift in range(1, size):
        perm = [(i, (i + shift) % size) for i in range(size)]
        piece = lax.dynamic_slice_in_dim(x, ((me + shift) % size) * chunk, chunk, 0)
        total = total + lax.ppermute(piece, axis_name, perm)
    return total


def body(hidden_states, w_query, w_key_value, adapter_down, adapter_up, req_lengths, req_adapter):
    dp_size = lax.axis_size("dp")
    row_size = lax.axis_size("row")
    col_size = lax.axis_size("col")
    block_index = lax.axis_index("dp")
    col_index = lax.axis_index("col")
    row_index = lax.axis_index("row")
    own_rows = hidden_states.shape[0]
    block_len = own_rows * row_size
    query_cols = w_query.shape[1]
    kv_cols = w_key_value.shape[1]
    kv_half = kv_cols // 2
    head_size = HEAD_DIM
    heads_here = query_cols // head_size
    heads_total = heads_here * row_size
    kv_heads = kv_half // head_size
    kv_group = row_index * heads_here // (heads_total // kv_heads)
    first_row = col_index * own_rows

    key_cols = lax.dynamic_slice_in_dim(w_key_value, kv_group * head_size, head_size, 1)
    value_cols = lax.dynamic_slice_in_dim(w_key_value, kv_half + kv_group * head_size, head_size, 1)
    weight_piece = jnp.concatenate([w_query, key_cols, value_cols], axis=1)
    weights_full = ring_gather(weight_piece, "col", 0)

    grid = [(a * col_size + b, b * col_size + a) for a in range(row_size) for b in range(col_size)]
    swapped = lax.ppermute(hidden_states, ("row", "col"), grid)
    own_inputs = ring_gather(swapped, "row", 1)

    held_sets = adapter_down.shape[0]
    width_here = adapter_down.shape[1]
    rank_size = adapter_down.shape[2]
    lengths_row = req_lengths[block_index]
    adapters_row = req_adapter[block_index]
    requests = lengths_row.shape[0]
    starts, segment, positions = block_layout(lengths_row, block_len)
    holders = adapters_row // held_sets
    request_ids = jnp.arange(requests, dtype=jnp.int32)
    token_holder = jnp.sum(
        jnp.where(segment[:, None] == request_ids[None, :] + 1, holders[None, :] + 1, 0), axis=1
    ) - 1
    wanted_from_me = (req_adapter // held_sets) == block_index
    local_pick = jnp.sum(jnp.where(wanted_from_me, req_adapter % held_sets, 0), axis=1)
    down_pick = jnp.transpose(jnp.take(adapter_down, local_pick, axis=0), (0, 2, 1))
    up_pick = jnp.take(adapter_up, local_pick, axis=0)
    outgoing = jnp.concatenate([down_pick, up_pick], axis=1)
    incoming = lax.all_to_all(outgoing, "dp", split_axis=0, concat_axis=0, tiled=True)
    flat_down = incoming[:, :rank_size, :].reshape(dp_size * rank_size, width_here).T
    flat_up = incoming[:, rank_size:, :].reshape(dp_size * rank_size, query_cols).astype(jnp.float32)
    slot_ids = jnp.arange(dp_size, dtype=jnp.int32)

    local_holder = lax.dynamic_slice_in_dim(token_holder, row_index * own_rows, own_rows, 0)
    reduced = jnp.dot(hidden_states, flat_down, preferred_element_type=jnp.float32)
    reduced = reduced.reshape(own_rows, dp_size, rank_size)
    local_mask = slot_ids[None, :] == local_holder[:, None]
    low_partial = jnp.sum(jnp.where(local_mask[:, :, None], reduced, 0.0), axis=1)
    low_swapped = lax.ppermute(low_partial, ("row", "col"), grid)
    low_rank = sum(shifted_copies(low_swapped, "row"))

    own_holder = lax.dynamic_slice_in_dim(token_holder, first_row, own_rows, 0)
    own_mask = slot_ids[None, :] == own_holder[:, None]
    spread = jnp.where(own_mask[:, :, None], low_rank[:, None, :], 0.0)
    spread = spread.reshape(own_rows, dp_size * rank_size)
    adapter_term = jnp.dot(spread, flat_up, precision=lax.Precision.HIGHEST)

    query_rows = (
        jnp.dot(own_inputs, weights_full[:, :query_cols], preferred_element_type=jnp.float32)
        + adapter_term
    ).astype(jnp.bfloat16)
    head_kv = jnp.dot(
        own_inputs, weights_full[:, query_cols:], preferred_element_type=jnp.float32
    ).astype(jnp.bfloat16)

    partner = [(i, (i + row_size // kv_heads) % row_size) for i in range(row_size)]
    other_kv = lax.ppermute(head_kv, "row", partner)
    first_is_own = kv_group == 0
    low_head = jnp.where(first_is_own, head_kv, other_kv)
    high_head = jnp.where(first_is_own, other_kv, head_kv)
    kv_cache = jnp.concatenate(
        [low_head[:, :head_size], high_head[:, :head_size], low_head[:, head_size:], high_head[:, head_size:]],
        axis=1,
    )

    attend, initial = make_attend(query_rows, segment, first_row, 0, head_size, head_size)
    running_max, running_sum, running_out = attend(
        initial, ring_gather(head_kv, "col", 0), jnp.int32(0)
    )
    attention = (running_out / running_sum[:, :, None]).astype(jnp.bfloat16)
    attention = jnp.transpose(attention, (1, 0, 2)).reshape(own_rows, query_cols)
    return (attention, kv_cache)


def solution(mesh):
    return jax.shard_map(
        body,
        mesh=mesh,
        in_specs=(
            P(("dp", "row"), "col"),
            P("col", "row"),
            P("col", None),
            P("dp", "col", None),
            P("dp", None, "row"),
            P(),
            P(),
        ),
        out_specs=(P(("dp", "col"), "row"), P(("dp", "col"), None)),
        check_vma=False,
    )
```

```python
import math

import jax
import jax.numpy as jnp
from jax import lax
from jax.sharding import PartitionSpec as P

HEAD_DIM = 128
MOST_LEN = 160


masked_score = -1e30


def block_layout(lengths_row, block_len):
    prefix_len = block_len - jnp.sum(lengths_row)
    ends_at = jnp.cumsum(lengths_row) + prefix_len
    starts = ends_at - lengths_row
    positions = jnp.arange(block_len, dtype=jnp.int32)
    segment = jnp.sum((positions[:, None] >= starts[None, :]).astype(jnp.int32), axis=1)
    return (starts, segment, positions)


def slot_numbers(holders):
    request_total = holders.shape[0]
    ordering = jnp.arange(request_total, dtype=jnp.int32)
    earlier = ordering[None, :] < ordering[:, None]
    same_holder = holders[:, None] == holders[None, :]
    return jnp.sum((earlier & same_holder).astype(jnp.int32), axis=1)


def make_attend(query_rows, segment, first_row, kv_group, head_size, kv_half):
    own_rows = query_rows.shape[0]
    heads_here = query_rows.shape[1] // head_size
    query_heads = query_rows.reshape(own_rows, heads_here, head_size)
    query_pos = first_row + jnp.arange(own_rows, dtype=jnp.int32)
    query_seg = lax.dynamic_slice_in_dim(segment, first_row, own_rows, 0)
    score_scale = 1.0 / math.sqrt(head_size)

    def attend(state_in, key_block, key_start):
        running_max, running_sum, running_out = state_in
        block_size = key_block.shape[0]
        key_rows = lax.dynamic_slice_in_dim(key_block, kv_group * head_size, head_size, 1)
        values = lax.dynamic_slice_in_dim(key_block, kv_half + kv_group * head_size, head_size, 1)
        key_pos = jnp.arange(block_size, dtype=jnp.int32)
        allowed = (key_pos[None, :] <= query_pos[:, None]) & (
            (segment[None, :] == query_seg[:, None]) | (segment[None, :] == 0)
        )
        scores = (
            jnp.einsum("qhd,kd->hqk", query_heads, key_rows, preferred_element_type=jnp.float32)
            * score_scale
        )
        scores = jnp.where(allowed[None], scores, masked_score)
        new_max = jnp.maximum(running_max, jnp.max(scores, axis=2))
        weights = jnp.where(allowed[None], jnp.exp(scores - new_max[:, :, None]), 0.0)
        running_sum = jnp.sum(weights, axis=2)
        running_out = jnp.einsum(
            "hqk,kd->hqd", weights.astype(jnp.bfloat16), values, preferred_element_type=jnp.float32
        )
        return (new_max, running_sum, running_out)

    initial = (
        jnp.full((heads_here, own_rows), masked_score, jnp.float32),
        jnp.zeros((heads_here, own_rows), jnp.float32),
        jnp.zeros((heads_here, own_rows, head_size), jnp.float32),
    )
    return (attend, initial)


def shifted_copies(x, axis_name):
    size = lax.axis_size(axis_name)
    copies = [x]
    for shift in range(1, size):
        perm = [(i, (i - shift) % size) for i in range(size)]
        copies.append(lax.ppermute(x, axis_name, perm))
    return copies


def ring_gather(x, axis_name, axis):
    size = lax.axis_size(axis_name)
    me = lax.axis_index(axis_name)
    copies = shifted_copies(x, axis_name)
    doubled = jnp.stack(copies + copies, axis=0)
    ordered = lax.dynamic_slice_in_dim(doubled, size - me, size, 0)
    moved = jnp.moveaxis(ordered, 0, axis)
    shape = list(x.shape)
    shape[axis] = shape[axis] * size
    return moved.reshape(shape)


def ring_reduce_scatter(x, axis_name):
    size = lax.axis_size(axis_name)
    me = lax.axis_index(axis_name)
    chunk = x.shape[0] // size
    total = lax.dynamic_slice_in_dim(x, me * chunk, chunk, 0)
    for shift in range(1, size):
        perm = [(i, (i + shift) % size) for i in range(size)]
        piece = lax.dynamic_slice_in_dim(x, ((me + shift) % size) * chunk, chunk, 0)
        total = total + lax.ppermute(piece, axis_name, perm)
    return total


def spread_rows(x, row_size, col_size):
    me = lax.axis_index("row")
    copies = []
    for shift in range(row_size):
        pairs = [
            (a * col_size + b, ((b - shift) % row_size) * col_size + a)
            for a in range(row_size)
            for b in range(col_size)
        ]
        copies.append(lax.ppermute(x, ("row", "col"), pairs))
    doubled = jnp.stack(copies + copies, axis=0)
    return lax.dynamic_slice_in_dim(doubled, row_size - me, row_size, 0)


def core_shared_gather(piece, axis_name):
    size = lax.axis_size(axis_name)
    me = lax.axis_index(axis_name)
    core = lax.axis_index("dp") % 2
    half = piece.shape[0] // 2
    mine = lax.dynamic_slice_in_dim(piece, core * half, half, 0)
    fetched = []
    for shift in range(1, size):
        perm = [(i, (i - shift) % size) for i in range(size)]
        fetched.append(lax.ppermute(mine, axis_name, perm))
    fetched = jnp.stack(fetched, axis=0)
    dp_size = lax.axis_size("dp")
    swap = [(i, i ^ 1) for i in range(dp_size)]
    partner = lax.ppermute(fetched, "dp", swap)
    first = jnp.where(core == 0, fetched, partner)
    second = jnp.where(core == 0, partner, fetched)
    remote = jnp.concatenate([first, second], axis=1)
    copies = jnp.concatenate([piece[None], remote], axis=0)
    doubled = jnp.concatenate([copies, copies], axis=0)
    ordered = lax.dynamic_slice_in_dim(doubled, size - me, size, 0)
    return ordered.reshape((size * piece.shape[0],) + piece.shape[1:])


def body(hidden_states, w_query, w_key_value, adapter_down, adapter_up, req_lengths, req_adapter):
    dp_size = lax.axis_size("dp")
    row_size = lax.axis_size("row")
    col_size = lax.axis_size("col")
    block_index = lax.axis_index("dp")
    col_index = lax.axis_index("col")
    row_index = lax.axis_index("row")
    own_rows = hidden_states.shape[0]
    block_len = own_rows * row_size
    query_cols = w_query.shape[1]
    kv_cols = w_key_value.shape[1]
    kv_half = kv_cols // 2
    head_size = HEAD_DIM
    heads_here = query_cols // head_size
    heads_total = heads_here * row_size
    kv_heads = kv_half // head_size
    kv_group = row_index * heads_here // (heads_total // kv_heads)
    first_row = col_index * own_rows

    key_cols = lax.dynamic_slice_in_dim(w_key_value, kv_group * head_size, head_size, 1)
    value_cols = lax.dynamic_slice_in_dim(w_key_value, kv_half + kv_group * head_size, head_size, 1)
    weight_piece = jnp.concatenate([w_query, key_cols, value_cols], axis=1)
    weights_full = core_shared_gather(weight_piece, "col")

    own_inputs = spread_rows(hidden_states, row_size, col_size)
    own_inputs = jnp.moveaxis(own_inputs, 0, 1).reshape(own_rows, row_size * hidden_states.shape[1])

    held_sets = adapter_down.shape[0]
    width_here = adapter_down.shape[1]
    rank_size = adapter_down.shape[2]
    lengths_row = req_lengths[block_index]
    adapters_row = req_adapter[block_index]
    requests = lengths_row.shape[0]
    starts, segment, positions = block_layout(lengths_row, block_len)
    holders = adapters_row // held_sets
    request_ids = jnp.arange(requests, dtype=jnp.int32)
    token_holder = jnp.sum(
        jnp.where(segment[:, None] == request_ids[None, :] + 1, holders[None, :] + 1, 0), axis=1
    ) - 1
    wanted_from_me = (req_adapter // held_sets) == block_index
    local_pick = jnp.sum(jnp.where(wanted_from_me, req_adapter % held_sets, 0), axis=1)
    down_pick = jnp.transpose(jnp.take(adapter_down, local_pick, axis=0), (0, 2, 1))
    up_pick = jnp.take(adapter_up, local_pick, axis=0)
    outgoing = jnp.concatenate([down_pick, up_pick], axis=1)
    incoming = lax.all_to_all(outgoing, "dp", split_axis=0, concat_axis=0, tiled=True)
    flat_down = incoming[:, :rank_size, :].reshape(dp_size * rank_size, width_here).T
    flat_up = incoming[:, rank_size:, :].reshape(dp_size * rank_size, query_cols).astype(jnp.float32)
    slot_ids = jnp.arange(dp_size, dtype=jnp.int32)

    local_holder = lax.dynamic_slice_in_dim(token_holder, row_index * own_rows, own_rows, 0)
    reduced = jnp.dot(hidden_states, flat_down, preferred_element_type=jnp.float32)
    reduced = reduced.reshape(own_rows, dp_size, rank_size)
    local_mask = slot_ids[None, :] == local_holder[:, None]
    low_partial = jnp.sum(jnp.where(local_mask[:, :, None], reduced, 0.0), axis=1)
    low_rank = jnp.sum(spread_rows(low_partial, row_size, col_size), axis=0)

    own_holder = lax.dynamic_slice_in_dim(token_holder, first_row, own_rows, 0)
    own_mask = slot_ids[None, :] == own_holder[:, None]
    spread = jnp.where(own_mask[:, :, None], low_rank[:, None, :], 0.0)
    spread = spread.reshape(own_rows, dp_size * rank_size)
    adapter_term = jnp.dot(spread, flat_up, precision=lax.Precision.HIGHEST)

    query_rows = (
        jnp.dot(own_inputs, weights_full[:, :query_cols], preferred_element_type=jnp.float32)
        + adapter_term
    ).astype(jnp.bfloat16)
    head_kv = jnp.dot(
        own_inputs, weights_full[:, query_cols:], preferred_element_type=jnp.float32
    ).astype(jnp.bfloat16)

    partner = [(i, (i + row_size // kv_heads) % row_size) for i in range(row_size)]
    other_kv = lax.ppermute(head_kv, "row", partner)
    first_is_own = kv_group == 0
    low_head = jnp.where(first_is_own, head_kv, other_kv)
    high_head = jnp.where(first_is_own, other_kv, head_kv)
    kv_cache = jnp.concatenate(
        [low_head[:, :head_size], high_head[:, :head_size], low_head[:, head_size:], high_head[:, head_size:]],
        axis=1,
    )

    attend, initial = make_attend(query_rows, segment, first_row, 0, head_size, head_size)
    running_max, running_sum, running_out = attend(
        initial, ring_gather(head_kv, "col", 0), jnp.int32(0)
    )
    attention = (running_out / running_sum[:, :, None]).astype(jnp.bfloat16)
    attention = jnp.transpose(attention, (1, 0, 2)).reshape(own_rows, query_cols)
    return (attention, kv_cache)


def solution(mesh):
    return jax.shard_map(
        body,
        mesh=mesh,
        in_specs=(
            P(("dp", "row"), "col"),
            P("col", "row"),
            P("col", None),
            P("dp", "col", None),
            P("dp", None, "row"),
            P(),
            P(),
        ),
        out_specs=(P(("dp", "col"), "row"), P(("dp", "col"), None)),
        check_vma=False,
    )
```

```python
import math

import jax
import jax.numpy as jnp
from jax import lax
from jax.sharding import PartitionSpec as P

HEAD_DIM = 128
MOST_LEN = 160


masked_score = -1e30


def block_layout(lengths_row, block_len):
    prefix_len = block_len - jnp.sum(lengths_row)
    ends_at = jnp.cumsum(lengths_row) + prefix_len
    starts = ends_at - lengths_row
    positions = jnp.arange(block_len, dtype=jnp.int32)
    segment = jnp.sum((positions[:, None] >= starts[None, :]).astype(jnp.int32), axis=1)
    return (starts, segment, positions)


def slot_numbers(holders):
    request_total = holders.shape[0]
    ordering = jnp.arange(request_total, dtype=jnp.int32)
    earlier = ordering[None, :] < ordering[:, None]
    same_holder = holders[:, None] == holders[None, :]
    return jnp.sum((earlier & same_holder).astype(jnp.int32), axis=1)


def make_attend(query_rows, segment, first_row, kv_group, head_size, kv_half):
    own_rows = query_rows.shape[0]
    heads_here = query_rows.shape[1] // head_size
    query_heads = query_rows.reshape(own_rows, heads_here, head_size)
    query_pos = first_row + jnp.arange(own_rows, dtype=jnp.int32)
    query_seg = lax.dynamic_slice_in_dim(segment, first_row, own_rows, 0)
    score_scale = 1.0 / math.sqrt(head_size)

    def attend(state_in, key_block, key_start):
        running_max, running_sum, running_out = state_in
        block_size = key_block.shape[0]
        key_rows = lax.dynamic_slice_in_dim(key_block, kv_group * head_size, head_size, 1)
        values = lax.dynamic_slice_in_dim(key_block, kv_half + kv_group * head_size, head_size, 1)
        key_pos = jnp.arange(block_size, dtype=jnp.int32)
        allowed = (key_pos[None, :] <= query_pos[:, None]) & (
            (segment[None, :] == query_seg[:, None]) | (segment[None, :] == 0)
        )
        scores = (
            jnp.einsum("qhd,kd->hqk", query_heads, key_rows, preferred_element_type=jnp.float32)
            * score_scale
        )
        scores = jnp.where(allowed[None], scores, masked_score)
        new_max = jnp.maximum(running_max, jnp.max(scores, axis=2))
        weights = jnp.where(allowed[None], jnp.exp(scores - new_max[:, :, None]), 0.0)
        running_sum = jnp.sum(weights, axis=2)
        running_out = jnp.einsum(
            "hqk,kd->hqd", weights.astype(jnp.bfloat16), values, preferred_element_type=jnp.float32
        )
        return (new_max, running_sum, running_out)

    initial = (
        jnp.full((heads_here, own_rows), masked_score, jnp.float32),
        jnp.zeros((heads_here, own_rows), jnp.float32),
        jnp.zeros((heads_here, own_rows, head_size), jnp.float32),
    )
    return (attend, initial)


def shifted_copies(x, axis_name):
    size = lax.axis_size(axis_name)
    copies = [x]
    for shift in range(1, size):
        perm = [(i, (i - shift) % size) for i in range(size)]
        copies.append(lax.ppermute(x, axis_name, perm))
    return copies


def ring_gather(x, axis_name, axis):
    size = lax.axis_size(axis_name)
    me = lax.axis_index(axis_name)
    copies = shifted_copies(x, axis_name)
    doubled = jnp.stack(copies + copies, axis=0)
    ordered = lax.dynamic_slice_in_dim(doubled, size - me, size, 0)
    moved = jnp.moveaxis(ordered, 0, axis)
    shape = list(x.shape)
    shape[axis] = shape[axis] * size
    return moved.reshape(shape)


def ring_reduce_scatter(x, axis_name):
    size = lax.axis_size(axis_name)
    me = lax.axis_index(axis_name)
    chunk = x.shape[0] // size
    total = lax.dynamic_slice_in_dim(x, me * chunk, chunk, 0)
    for shift in range(1, size):
        perm = [(i, (i + shift) % size) for i in range(size)]
        piece = lax.dynamic_slice_in_dim(x, ((me + shift) % size) * chunk, chunk, 0)
        total = total + lax.ppermute(piece, axis_name, perm)
    return total


def spread_rows(x, row_size, col_size):
    me = lax.axis_index("row")
    copies = []
    for shift in range(row_size):
        pairs = [
            (a * col_size + b, ((b - shift) % row_size) * col_size + a)
            for a in range(row_size)
            for b in range(col_size)
        ]
        copies.append(lax.ppermute(x, ("row", "col"), pairs))
    doubled = jnp.stack(copies + copies, axis=0)
    return lax.dynamic_slice_in_dim(doubled, row_size - me, row_size, 0)


def core_shared_gather(piece, extra, axis_name):
    size = lax.axis_size(axis_name)
    me = lax.axis_index(axis_name)
    core = lax.axis_index("dp") % 2
    half = piece.shape[0] // 2
    mine = lax.dynamic_slice_in_dim(piece, core * half, half, 0)
    extra_rows = extra.reshape(half, -1)
    sent = jnp.concatenate([mine, extra_rows], axis=1)
    fetched = []
    for shift in range(1, size):
        perm = [(i, (i - shift) % size) for i in range(size)]
        fetched.append(lax.ppermute(sent, axis_name, perm))
    fetched = jnp.stack(fetched, axis=0)
    width = piece.shape[1]
    fetched_piece = fetched[:, :, :width]
    fetched_extra = fetched[:, :, width:].reshape((size - 1,) + extra.shape)
    dp_size = lax.axis_size("dp")
    swap = [(i, i ^ 1) for i in range(dp_size)]
    partner = lax.ppermute(fetched_piece, "dp", swap)
    first = jnp.where(core == 0, fetched_piece, partner)
    second = jnp.where(core == 0, partner, fetched_piece)
    remote = jnp.concatenate([first, second], axis=1)

    def in_order(own, others):
        copies = jnp.concatenate([own[None], others], axis=0)
        doubled = jnp.concatenate([copies, copies], axis=0)
        ordered = lax.dynamic_slice_in_dim(doubled, size - me, size, 0)
        return ordered.reshape((size * own.shape[0],) + own.shape[1:])

    return in_order(piece, remote), in_order(extra, fetched_extra)


def body(hidden_states, w_query, w_key_value, adapter_down, adapter_up, req_lengths, req_adapter):
    dp_size = lax.axis_size("dp")
    row_size = lax.axis_size("row")
    col_size = lax.axis_size("col")
    block_index = lax.axis_index("dp")
    col_index = lax.axis_index("col")
    row_index = lax.axis_index("row")
    own_rows = hidden_states.shape[0]
    block_len = own_rows * row_size
    query_cols = w_query.shape[1]
    kv_cols = w_key_value.shape[1]
    kv_half = kv_cols // 2
    head_size = HEAD_DIM
    heads_here = query_cols // head_size
    heads_total = heads_here * row_size
    kv_heads = kv_half // head_size
    kv_group = row_index * heads_here // (heads_total // kv_heads)
    first_row = col_index * own_rows

    key_cols = lax.dynamic_slice_in_dim(w_key_value, kv_group * head_size, head_size, 1)
    value_cols = lax.dynamic_slice_in_dim(w_key_value, kv_half + kv_group * head_size, head_size, 1)
    weight_piece = jnp.concatenate([w_query, key_cols, value_cols], axis=1)

    own_inputs = spread_rows(hidden_states, row_size, col_size)
    own_inputs = jnp.moveaxis(own_inputs, 0, 1).reshape(own_rows, row_size * hidden_states.shape[1])

    held_sets = adapter_down.shape[0]
    width_here = adapter_down.shape[1]
    rank_size = adapter_down.shape[2]
    lengths_row = req_lengths[block_index]
    adapters_row = req_adapter[block_index]
    requests = lengths_row.shape[0]
    starts, segment, positions = block_layout(lengths_row, block_len)
    holders = adapters_row // held_sets
    request_ids = jnp.arange(requests, dtype=jnp.int32)
    token_holder = jnp.sum(
        jnp.where(segment[:, None] == request_ids[None, :] + 1, holders[None, :] + 1, 0), axis=1
    ) - 1
    wanted_from_me = (req_adapter // held_sets) == block_index
    local_pick = jnp.sum(jnp.where(wanted_from_me, req_adapter % held_sets, 0), axis=1)
    down_pick = jnp.transpose(jnp.take(adapter_down, local_pick, axis=0), (0, 2, 1))
    up_pick = jnp.take(adapter_up, local_pick, axis=0)
    outgoing = jnp.concatenate([down_pick, up_pick], axis=1)
    incoming = lax.all_to_all(outgoing, "dp", split_axis=0, concat_axis=0, tiled=True)
    flat_down = incoming[:, :rank_size, :].reshape(dp_size * rank_size, width_here).T
    flat_up = incoming[:, rank_size:, :].reshape(dp_size * rank_size, query_cols).astype(jnp.float32)
    slot_ids = jnp.arange(dp_size, dtype=jnp.int32)

    weights_full, down_full = core_shared_gather(weight_piece, flat_down, "col")
    low_rank = jnp.dot(own_inputs, down_full, preferred_element_type=jnp.float32)

    own_holder = lax.dynamic_slice_in_dim(token_holder, first_row, own_rows, 0)
    own_mask = slot_ids[None, :] == own_holder[:, None]
    low_rank = low_rank.reshape(own_rows, dp_size, rank_size)
    spread = jnp.where(own_mask[:, :, None], low_rank, 0.0)
    spread = spread.reshape(own_rows, dp_size * rank_size)
    adapter_term = jnp.dot(spread, flat_up, precision=lax.Precision.HIGHEST)

    query_rows = (
        jnp.dot(own_inputs, weights_full[:, :query_cols], preferred_element_type=jnp.float32)
        + adapter_term
    ).astype(jnp.bfloat16)
    head_kv = jnp.dot(
        own_inputs, weights_full[:, query_cols:], preferred_element_type=jnp.float32
    ).astype(jnp.bfloat16)

    partner = [(i, (i + row_size // kv_heads) % row_size) for i in range(row_size)]
    other_kv = lax.ppermute(head_kv, "row", partner)
    first_is_own = kv_group == 0
    low_head = jnp.where(first_is_own, head_kv, other_kv)
    high_head = jnp.where(first_is_own, other_kv, head_kv)
    kv_cache = jnp.concatenate(
        [low_head[:, :head_size], high_head[:, :head_size], low_head[:, head_size:], high_head[:, head_size:]],
        axis=1,
    )

    attend, initial = make_attend(query_rows, segment, first_row, 0, head_size, head_size)
    running_max, running_sum, running_out = attend(
        initial, ring_gather(head_kv, "col", 0), jnp.int32(0)
    )
    attention = (running_out / running_sum[:, :, None]).astype(jnp.bfloat16)
    attention = jnp.transpose(attention, (1, 0, 2)).reshape(own_rows, query_cols)
    return (attention, kv_cache)


def solution(mesh):
    return jax.shard_map(
        body,
        mesh=mesh,
        in_specs=(
            P(("dp", "row"), "col"),
            P("col", "row"),
            P("col", None),
            P("dp", "col", None),
            P("dp", None, "row"),
            P(),
            P(),
        ),
        out_specs=(P(("dp", "col"), "row"), P(("dp", "col"), None)),
        check_vma=False,
    )
```

```python
import math

import jax
import jax.numpy as jnp
from jax import lax
from jax.sharding import PartitionSpec as P


HEAD_DIM = 128


masked_score = -1e30


def block_layout(lengths_row, block_len):
    prefix_len = block_len - jnp.sum(lengths_row)
    ends_at = jnp.cumsum(lengths_row) + prefix_len
    starts = ends_at - lengths_row
    positions = jnp.arange(block_len, dtype=jnp.int32)
    segment = jnp.sum((positions[:, None] >= starts[None, :]).astype(jnp.int32), axis=1)
    return (starts, segment, positions)


def make_attend(query_rows, segment, first_row, kv_group, head_size, kv_half):
    own_rows = query_rows.shape[0]
    heads_here = query_rows.shape[1] // head_size
    query_heads = query_rows.reshape(own_rows, heads_here, head_size)
    query_pos = first_row + jnp.arange(own_rows, dtype=jnp.int32)
    query_seg = lax.dynamic_slice_in_dim(segment, first_row, own_rows, 0)
    score_scale = 1.0 / math.sqrt(head_size)

    def attend(state_in, key_block, key_start):
        running_max, running_sum, running_out = state_in
        block_size = key_block.shape[0]
        key_rows = lax.dynamic_slice_in_dim(key_block, kv_group * head_size, head_size, 1)
        values = lax.dynamic_slice_in_dim(key_block, kv_half + kv_group * head_size, head_size, 1)
        key_pos = jnp.arange(block_size, dtype=jnp.int32)
        allowed = (key_pos[None, :] <= query_pos[:, None]) & (
            (segment[None, :] == query_seg[:, None]) | (segment[None, :] == 0)
        )
        scores = (
            jnp.einsum("qhd,kd->hqk", query_heads, key_rows, preferred_element_type=jnp.float32)
            * score_scale
        )
        scores = jnp.where(allowed[None], scores, masked_score)
        new_max = jnp.maximum(running_max, jnp.max(scores, axis=2))
        weights = jnp.where(allowed[None], jnp.exp(scores - new_max[:, :, None]), 0.0)
        running_sum = jnp.sum(weights, axis=2)
        running_out = jnp.einsum(
            "hqk,kd->hqd", weights.astype(jnp.bfloat16), values, preferred_element_type=jnp.float32
        )
        return (new_max, running_sum, running_out)

    initial = (
        jnp.full((heads_here, own_rows), masked_score, jnp.float32),
        jnp.zeros((heads_here, own_rows), jnp.float32),
        jnp.zeros((heads_here, own_rows, head_size), jnp.float32),
    )
    return (attend, initial)


def shifted_copies(x, axis_name):
    size = lax.axis_size(axis_name)
    copies = [x]
    for shift in range(1, size):
        perm = [(i, (i - shift) % size) for i in range(size)]
        copies.append(lax.ppermute(x, axis_name, perm))
    return copies


def ring_gather(x, axis_name, axis):
    size = lax.axis_size(axis_name)
    me = lax.axis_index(axis_name)
    copies = shifted_copies(x, axis_name)
    doubled = jnp.stack(copies + copies, axis=0)
    ordered = lax.dynamic_slice_in_dim(doubled, size - me, size, 0)
    moved = jnp.moveaxis(ordered, 0, axis)
    shape = list(x.shape)
    shape[axis] = shape[axis] * size
    return moved.reshape(shape)


def spread_rows(x, row_size, col_size):
    me = lax.axis_index("row")
    copies = []
    for shift in range(row_size):
        pairs = [
            (a * col_size + b, ((b - shift) % row_size) * col_size + a)
            for a in range(row_size)
            for b in range(col_size)
        ]
        copies.append(lax.ppermute(x, ("row", "col"), pairs))
    doubled = jnp.stack(copies + copies, axis=0)
    return lax.dynamic_slice_in_dim(doubled, row_size - me, row_size, 0)


def core_shared_gather(piece, axis_name):
    size = lax.axis_size(axis_name)
    me = lax.axis_index(axis_name)
    core = lax.axis_index("dp") % 2
    half = piece.shape[0] // 2
    mine = lax.dynamic_slice_in_dim(piece, core * half, half, 0)
    fetched = []
    for shift in range(1, size):
        perm = [(i, (i - shift) % size) for i in range(size)]
        fetched.append(lax.ppermute(mine, axis_name, perm))
    fetched = jnp.stack(fetched, axis=0)
    dp_size = lax.axis_size("dp")
    swap = [(i, i ^ 1) for i in range(dp_size)]
    partner = lax.ppermute(fetched, "dp", swap)
    first = jnp.where(core == 0, fetched, partner)
    second = jnp.where(core == 0, partner, fetched)
    remote = jnp.concatenate([first, second], axis=1)
    copies = jnp.concatenate([piece[None], remote], axis=0)
    doubled = jnp.concatenate([copies, copies], axis=0)
    ordered = lax.dynamic_slice_in_dim(doubled, size - me, size, 0)
    return ordered.reshape((size * piece.shape[0],) + piece.shape[1:])


def body(hidden_states, w_query, w_key_value, adapter_down, adapter_up, req_lengths, req_adapter):
    dp_size = lax.axis_size("dp")
    row_size = lax.axis_size("row")
    col_size = lax.axis_size("col")
    block_index = lax.axis_index("dp")
    col_index = lax.axis_index("col")
    row_index = lax.axis_index("row")
    own_rows = hidden_states.shape[0]
    block_len = own_rows * row_size
    query_cols = w_query.shape[1]
    kv_cols = w_key_value.shape[1]
    kv_half = kv_cols // 2
    head_size = HEAD_DIM
    heads_here = query_cols // head_size
    heads_total = heads_here * row_size
    kv_heads = kv_half // head_size
    kv_group = row_index * heads_here // (heads_total // kv_heads)
    first_row = col_index * own_rows

    key_cols = lax.dynamic_slice_in_dim(w_key_value, kv_group * head_size, head_size, 1)
    value_cols = lax.dynamic_slice_in_dim(w_key_value, kv_half + kv_group * head_size, head_size, 1)
    weight_piece = jnp.concatenate([w_query, key_cols, value_cols], axis=1)
    weights_full = core_shared_gather(weight_piece, "col")

    own_inputs = spread_rows(hidden_states, row_size, col_size)
    own_inputs = jnp.moveaxis(own_inputs, 0, 1).reshape(own_rows, row_size * hidden_states.shape[1])

    held_sets = adapter_down.shape[0]
    width_here = adapter_down.shape[1]
    rank_size = adapter_down.shape[2]
    lengths_row = req_lengths[block_index]
    adapters_row = req_adapter[block_index]
    requests = lengths_row.shape[0]
    _, segment, _ = block_layout(lengths_row, block_len)
    holders = adapters_row // held_sets
    request_ids = jnp.arange(requests, dtype=jnp.int32)
    token_holder = jnp.sum(
        jnp.where(segment[:, None] == request_ids[None, :] + 1, holders[None, :] + 1, 0), axis=1
    ) - 1
    wanted_from_me = (req_adapter // held_sets) == block_index
    local_pick = jnp.sum(jnp.where(wanted_from_me, req_adapter % held_sets, 0), axis=1)
    down_pick = jnp.transpose(jnp.take(adapter_down, local_pick, axis=0), (0, 2, 1))
    up_pick = jnp.take(adapter_up, local_pick, axis=0)
    outgoing = jnp.concatenate([down_pick, up_pick], axis=1)
    incoming = lax.all_to_all(outgoing, "dp", split_axis=0, concat_axis=0, tiled=True)
    flat_down = incoming[:, :rank_size, :].reshape(dp_size * rank_size, width_here).T
    flat_up = incoming[:, rank_size:, :].reshape(dp_size * rank_size, query_cols).astype(jnp.float32)
    slot_ids = jnp.arange(dp_size, dtype=jnp.int32)

    local_holder = lax.dynamic_slice_in_dim(token_holder, row_index * own_rows, own_rows, 0)
    reduced = jnp.dot(hidden_states, flat_down, preferred_element_type=jnp.float32)
    reduced = reduced.reshape(own_rows, dp_size, rank_size)
    local_mask = slot_ids[None, :] == local_holder[:, None]
    low_partial = jnp.sum(jnp.where(local_mask[:, :, None], reduced, 0.0), axis=1)
    low_rank = jnp.sum(spread_rows(low_partial, row_size, col_size), axis=0)

    own_holder = lax.dynamic_slice_in_dim(token_holder, first_row, own_rows, 0)
    own_mask = slot_ids[None, :] == own_holder[:, None]
    spread = jnp.where(own_mask[:, :, None], low_rank[:, None, :], 0.0)
    spread = spread.reshape(own_rows, dp_size * rank_size)
    adapter_term = jnp.dot(spread, flat_up, precision=lax.Precision.HIGHEST)

    query_rows = (
        jnp.dot(own_inputs, weights_full[:, :query_cols], preferred_element_type=jnp.float32)
        + adapter_term
    ).astype(jnp.bfloat16)
    head_kv = jnp.dot(
        own_inputs, weights_full[:, query_cols:], preferred_element_type=jnp.float32
    ).astype(jnp.bfloat16)

    partner = [(i, (i + row_size // kv_heads) % row_size) for i in range(row_size)]
    other_kv = lax.ppermute(head_kv, "row", partner)
    key_values = ring_gather(head_kv, "col", 0)
    first_is_own = kv_group == 0
    low_head = jnp.where(first_is_own, head_kv, other_kv)
    high_head = jnp.where(first_is_own, other_kv, head_kv)
    kv_cache = jnp.concatenate(
        [low_head[:, :head_size], high_head[:, :head_size], low_head[:, head_size:], high_head[:, head_size:]],
        axis=1,
    )

    attend, initial = make_attend(query_rows, segment, first_row, 0, head_size, head_size)
    _, running_sum, running_out = attend(
        initial, key_values, jnp.int32(0)
    )
    attention = (running_out / running_sum[:, :, None]).astype(jnp.bfloat16)
    attention = jnp.transpose(attention, (1, 0, 2)).reshape(own_rows, query_cols)
    return (attention, kv_cache)


def solution(mesh):
    return jax.shard_map(
        body,
        mesh=mesh,
        in_specs=(
            P(("dp", "row"), "col"),
            P("col", "row"),
            P("col", None),
            P("dp", "col", None),
            P("dp", None, "row"),
            P(),
            P(),
        ),
        out_specs=(P(("dp", "col"), "row"), P(("dp", "col"), None)),
        check_vma=False,
    )
```

```python
import math

import jax
import jax.numpy as jnp
from jax import lax
from jax.sharding import PartitionSpec as P

HEAD_DIM = 128
MOST_LEN = 160


masked_score = -1e30


def block_layout(lengths_row, block_len):
    prefix_len = block_len - jnp.sum(lengths_row)
    ends_at = jnp.cumsum(lengths_row) + prefix_len
    starts = ends_at - lengths_row
    positions = jnp.arange(block_len, dtype=jnp.int32)
    segment = jnp.sum((positions[:, None] >= starts[None, :]).astype(jnp.int32), axis=1)
    return (starts, segment, positions)


def slot_numbers(holders):
    request_total = holders.shape[0]
    ordering = jnp.arange(request_total, dtype=jnp.int32)
    earlier = ordering[None, :] < ordering[:, None]
    same_holder = holders[:, None] == holders[None, :]
    return jnp.sum((earlier & same_holder).astype(jnp.int32), axis=1)


def make_attend(query_rows, segment, first_row, kv_group, head_size, kv_half):
    own_rows = query_rows.shape[0]
    heads_here = query_rows.shape[1] // head_size
    query_heads = query_rows.reshape(own_rows, heads_here, head_size)
    query_pos = first_row + jnp.arange(own_rows, dtype=jnp.int32)
    query_seg = lax.dynamic_slice_in_dim(segment, first_row, own_rows, 0)
    score_scale = 1.0 / math.sqrt(head_size)

    def attend(state_in, key_block, key_start):
        running_max, running_sum, running_out = state_in
        block_size = key_block.shape[0]
        key_rows = lax.dynamic_slice_in_dim(key_block, kv_group * head_size, head_size, 1)
        values = lax.dynamic_slice_in_dim(key_block, kv_half + kv_group * head_size, head_size, 1)
        key_pos = jnp.arange(block_size, dtype=jnp.int32)
        allowed = (key_pos[None, :] <= query_pos[:, None]) & (
            (segment[None, :] == query_seg[:, None]) | (segment[None, :] == 0)
        )
        scores = (
            jnp.einsum("qhd,kd->hqk", query_heads, key_rows, preferred_element_type=jnp.float32)
            * score_scale
        )
        scores = jnp.where(allowed[None], scores, masked_score)
        new_max = jnp.maximum(running_max, jnp.max(scores, axis=2))
        weights = jnp.where(allowed[None], jnp.exp(scores - new_max[:, :, None]), 0.0)
        running_sum = jnp.sum(weights, axis=2)
        running_out = jnp.einsum(
            "hqk,kd->hqd", weights.astype(jnp.bfloat16), values, preferred_element_type=jnp.float32
        )
        return (new_max, running_sum, running_out)

    initial = (
        jnp.full((heads_here, own_rows), masked_score, jnp.float32),
        jnp.zeros((heads_here, own_rows), jnp.float32),
        jnp.zeros((heads_here, own_rows, head_size), jnp.float32),
    )
    return (attend, initial)


def shifted_copies(x, axis_name):
    size = lax.axis_size(axis_name)
    copies = [x]
    for shift in range(1, size):
        perm = [(i, (i - shift) % size) for i in range(size)]
        copies.append(lax.ppermute(x, axis_name, perm))
    return copies


def ring_gather(x, axis_name, axis):
    size = lax.axis_size(axis_name)
    me = lax.axis_index(axis_name)
    copies = shifted_copies(x, axis_name)
    doubled = jnp.stack(copies + copies, axis=0)
    ordered = lax.dynamic_slice_in_dim(doubled, size - me, size, 0)
    moved = jnp.moveaxis(ordered, 0, axis)
    shape = list(x.shape)
    shape[axis] = shape[axis] * size
    return moved.reshape(shape)


def ring_reduce_scatter(x, axis_name):
    size = lax.axis_size(axis_name)
    me = lax.axis_index(axis_name)
    chunk = x.shape[0] // size
    total = lax.dynamic_slice_in_dim(x, me * chunk, chunk, 0)
    for shift in range(1, size):
        perm = [(i, (i + shift) % size) for i in range(size)]
        piece = lax.dynamic_slice_in_dim(x, ((me + shift) % size) * chunk, chunk, 0)
        total = total + lax.ppermute(piece, axis_name, perm)
    return total


def body(hidden_states, w_query, w_key_value, adapter_down, adapter_up, req_lengths, req_adapter):
    dp_size = lax.axis_size("dp")
    block_index = lax.axis_index("dp")
    col_index = lax.axis_index("col")
    row_index = lax.axis_index("row")
    gathered = ring_gather(hidden_states, "row", 0)
    block_len = gathered.shape[0]
    query_cols = w_query.shape[1]
    kv_cols = w_key_value.shape[1]
    kv_half = kv_cols // 2
    head_size = HEAD_DIM
    heads_here = query_cols // head_size
    heads_total = heads_here * lax.axis_size("row")
    kv_heads = kv_half // head_size
    kv_group = row_index * heads_here // (heads_total // kv_heads)
    own_rows = block_len // lax.axis_size("col")
    first_row = col_index * own_rows
    held_sets = adapter_down.shape[0]
    width_here = adapter_down.shape[1]
    rank_size = adapter_down.shape[2]
    lengths_row = req_lengths[block_index]
    adapters_row = req_adapter[block_index]
    requests = lengths_row.shape[0]
    starts, segment, positions = block_layout(lengths_row, block_len)
    request_of = jnp.clip(segment - 1, 0, requests - 1)
    in_request = segment > 0
    holders = adapters_row // held_sets
    wanted_from_me = (req_adapter // held_sets) == block_index
    local_pick = jnp.sum(jnp.where(wanted_from_me, req_adapter % held_sets, 0), axis=1)
    down_pick = jnp.transpose(jnp.take(adapter_down, local_pick, axis=0), (0, 2, 1))
    up_pick = jnp.take(adapter_up, local_pick, axis=0)
    outgoing = jnp.concatenate([down_pick, up_pick], axis=1)
    incoming = lax.all_to_all(outgoing, "dp", split_axis=0, concat_axis=0, tiled=True)
    flat_down = incoming[:, :rank_size, :].reshape(dp_size * rank_size, width_here).T
    flat_up = incoming[:, rank_size:, :].reshape(dp_size * rank_size, query_cols).astype(jnp.float32)
    reduced = jnp.dot(gathered, flat_down, preferred_element_type=jnp.float32)
    request_ids = jnp.arange(requests, dtype=jnp.int32)
    token_holder = jnp.sum(
        jnp.where(segment[:, None] == request_ids[None, :] + 1, holders[None, :] + 1, 0), axis=1
    ) - 1
    slot_ids = jnp.arange(dp_size, dtype=jnp.int32)
    token_mask = slot_ids[None, :] == token_holder[:, None]
    reduced = reduced.reshape(block_len, dp_size, rank_size)
    low_partial = jnp.sum(jnp.where(token_mask[:, :, None], reduced, 0.0), axis=1)
    low_rank = ring_reduce_scatter(low_partial, "col")
    own_mask = lax.dynamic_slice_in_dim(token_mask, first_row, own_rows, 0)
    spread = jnp.where(own_mask[:, :, None], low_rank[:, None, :], 0.0)
    spread = spread.reshape(own_rows, dp_size * rank_size)
    adapter_term = jnp.dot(spread, flat_up, precision=lax.Precision.HIGHEST)
    kv_share = kv_cols // lax.axis_size("row")
    kv_slice = lax.dynamic_slice_in_dim(w_key_value, row_index * kv_share, kv_share, 1)
    both_weights = jnp.concatenate([w_query, kv_slice], axis=1)
    partial_value = jnp.dot(gathered, both_weights, preferred_element_type=jnp.float32)
    summed = ring_reduce_scatter(partial_value, "col")
    query_rows = (summed[:, :query_cols] + adapter_term).astype(jnp.bfloat16)
    kv_cache = ring_gather(summed[:, query_cols:].astype(jnp.bfloat16), "row", 1)
    head_kv = jnp.concatenate(
        [
            lax.dynamic_slice_in_dim(kv_cache, kv_group * head_size, head_size, 1),
            lax.dynamic_slice_in_dim(kv_cache, kv_half + kv_group * head_size, head_size, 1),
        ],
        axis=1,
    )
    attend, initial = make_attend(query_rows, segment, first_row, 0, head_size, head_size)
    running_max, running_sum, running_out = attend(
        initial, ring_gather(head_kv, "col", 0), jnp.int32(0)
    )
    attention = (running_out / running_sum[:, :, None]).astype(jnp.bfloat16)
    attention = jnp.transpose(attention, (1, 0, 2)).reshape(own_rows, query_cols)
    return (attention, kv_cache)


def solution(mesh):
    return jax.shard_map(
        body,
        mesh=mesh,
        in_specs=(
            P(("dp", "row"), "col"),
            P("col", "row"),
            P("col", None),
            P("dp", "col", None),
            P("dp", None, "row"),
            P(),
            P(),
        ),
        out_specs=(P(("dp", "col"), "row"), P(("dp", "col"), None)),
        check_vma=False,
    )
```

```python
import math

import jax
import jax.numpy as jnp
from jax import lax
from jax.sharding import PartitionSpec as P

HEAD_DIM = 128
MOST_LEN = 160


masked_score = -1e30


def block_layout(lengths_row, block_len):
    prefix_len = block_len - jnp.sum(lengths_row)
    ends_at = jnp.cumsum(lengths_row) + prefix_len
    starts = ends_at - lengths_row
    positions = jnp.arange(block_len, dtype=jnp.int32)
    segment = jnp.sum((positions[:, None] >= starts[None, :]).astype(jnp.int32), axis=1)
    return (starts, segment, positions)


def slot_numbers(holders):
    request_total = holders.shape[0]
    ordering = jnp.arange(request_total, dtype=jnp.int32)
    earlier = ordering[None, :] < ordering[:, None]
    same_holder = holders[:, None] == holders[None, :]
    return jnp.sum((earlier & same_holder).astype(jnp.int32), axis=1)


def make_attend(query_rows, segment, first_row, kv_group, head_size, kv_half):
    own_rows = query_rows.shape[0]
    heads_here = query_rows.shape[1] // head_size
    query_heads = query_rows.reshape(own_rows, heads_here, head_size)
    query_pos = first_row + jnp.arange(own_rows, dtype=jnp.int32)
    query_seg = lax.dynamic_slice_in_dim(segment, first_row, own_rows, 0)
    score_scale = 1.0 / math.sqrt(head_size)

    def attend(state_in, key_block, key_start):
        running_max, running_sum, running_out = state_in
        block_size = key_block.shape[0]
        key_rows = lax.dynamic_slice_in_dim(key_block, kv_group * head_size, head_size, 1)
        values = lax.dynamic_slice_in_dim(key_block, kv_half + kv_group * head_size, head_size, 1)
        key_pos = jnp.arange(block_size, dtype=jnp.int32)
        allowed = (key_pos[None, :] <= query_pos[:, None]) & (
            (segment[None, :] == query_seg[:, None]) | (segment[None, :] == 0)
        )
        scores = (
            jnp.einsum("qhd,kd->hqk", query_heads, key_rows, preferred_element_type=jnp.float32)
            * score_scale
        )
        scores = jnp.where(allowed[None], scores, masked_score)
        new_max = jnp.maximum(running_max, jnp.max(scores, axis=2))
        weights = jnp.where(allowed[None], jnp.exp(scores - new_max[:, :, None]), 0.0)
        running_sum = jnp.sum(weights, axis=2)
        running_out = jnp.einsum(
            "hqk,kd->hqd", weights.astype(jnp.bfloat16), values, preferred_element_type=jnp.float32
        )
        return (new_max, running_sum, running_out)

    initial = (
        jnp.full((heads_here, own_rows), masked_score, jnp.float32),
        jnp.zeros((heads_here, own_rows), jnp.float32),
        jnp.zeros((heads_here, own_rows, head_size), jnp.float32),
    )
    return (attend, initial)


def shifted_copies(x, axis_name):
    size = lax.axis_size(axis_name)
    copies = [x]
    for shift in range(1, size):
        perm = [(i, (i - shift) % size) for i in range(size)]
        copies.append(lax.ppermute(x, axis_name, perm))
    return copies


def ring_gather(x, axis_name, axis):
    size = lax.axis_size(axis_name)
    me = lax.axis_index(axis_name)
    copies = shifted_copies(x, axis_name)
    doubled = jnp.stack(copies + copies, axis=0)
    ordered = lax.dynamic_slice_in_dim(doubled, size - me, size, 0)
    moved = jnp.moveaxis(ordered, 0, axis)
    shape = list(x.shape)
    shape[axis] = shape[axis] * size
    return moved.reshape(shape)


def ring_reduce_scatter(x, axis_name, wire_dtype=None):
    size = lax.axis_size(axis_name)
    me = lax.axis_index(axis_name)
    chunk = x.shape[0] // size
    total = lax.dynamic_slice_in_dim(x, me * chunk, chunk, 0)
    for shift in range(1, size):
        perm = [(i, (i + shift) % size) for i in range(size)]
        piece = lax.dynamic_slice_in_dim(x, ((me + shift) % size) * chunk, chunk, 0)
        if wire_dtype is not None:
            piece = piece.astype(wire_dtype)
        total = total + lax.ppermute(piece, axis_name, perm).astype(x.dtype)
    return total


def body(hidden_states, w_query, w_key_value, adapter_down, adapter_up, req_lengths, req_adapter):
    dp_size = lax.axis_size("dp")
    block_index = lax.axis_index("dp")
    col_index = lax.axis_index("col")
    row_index = lax.axis_index("row")
    gathered = ring_gather(hidden_states, "row", 0)
    block_len = gathered.shape[0]
    query_cols = w_query.shape[1]
    kv_cols = w_key_value.shape[1]
    kv_half = kv_cols // 2
    head_size = HEAD_DIM
    heads_here = query_cols // head_size
    heads_total = heads_here * lax.axis_size("row")
    kv_heads = kv_half // head_size
    kv_group = row_index * heads_here // (heads_total // kv_heads)
    own_rows = block_len // lax.axis_size("col")
    first_row = col_index * own_rows
    held_sets = adapter_down.shape[0]
    width_here = adapter_down.shape[1]
    rank_size = adapter_down.shape[2]
    lengths_row = req_lengths[block_index]
    adapters_row = req_adapter[block_index]
    requests = lengths_row.shape[0]
    starts, segment, positions = block_layout(lengths_row, block_len)
    request_of = jnp.clip(segment - 1, 0, requests - 1)
    in_request = segment > 0
    holders = adapters_row // held_sets
    wanted_from_me = (req_adapter // held_sets) == block_index
    local_pick = jnp.sum(jnp.where(wanted_from_me, req_adapter % held_sets, 0), axis=1)
    down_pick = jnp.transpose(jnp.take(adapter_down, local_pick, axis=0), (0, 2, 1))
    up_pick = jnp.take(adapter_up, local_pick, axis=0)
    outgoing = jnp.concatenate([down_pick, up_pick], axis=1)
    incoming = lax.all_to_all(outgoing, "dp", split_axis=0, concat_axis=0, tiled=True)
    flat_down = incoming[:, :rank_size, :].reshape(dp_size * rank_size, width_here).T
    flat_up = incoming[:, rank_size:, :].reshape(dp_size * rank_size, query_cols).astype(jnp.float32)
    reduced = jnp.dot(gathered, flat_down, preferred_element_type=jnp.float32)
    request_ids = jnp.arange(requests, dtype=jnp.int32)
    token_holder = jnp.sum(
        jnp.where(segment[:, None] == request_ids[None, :] + 1, holders[None, :] + 1, 0), axis=1
    ) - 1
    slot_ids = jnp.arange(dp_size, dtype=jnp.int32)
    token_mask = slot_ids[None, :] == token_holder[:, None]
    reduced = reduced.reshape(block_len, dp_size, rank_size)
    low_partial = jnp.sum(jnp.where(token_mask[:, :, None], reduced, 0.0), axis=1)
    low_rank = ring_reduce_scatter(low_partial, "col")
    own_mask = lax.dynamic_slice_in_dim(token_mask, first_row, own_rows, 0)
    spread = jnp.where(own_mask[:, :, None], low_rank[:, None, :], 0.0)
    spread = spread.reshape(own_rows, dp_size * rank_size)
    adapter_term = jnp.dot(spread, flat_up, precision=lax.Precision.HIGHEST)
    kv_share = kv_cols // lax.axis_size("row")
    kv_slice = lax.dynamic_slice_in_dim(w_key_value, row_index * kv_share, kv_share, 1)
    both_weights = jnp.concatenate([w_query, kv_slice], axis=1)
    partial_value = jnp.dot(gathered, both_weights, preferred_element_type=jnp.float32)
    summed = ring_reduce_scatter(partial_value, "col", jnp.bfloat16)
    query_rows = (summed[:, :query_cols] + adapter_term).astype(jnp.bfloat16)
    kv_cache = ring_gather(summed[:, query_cols:].astype(jnp.bfloat16), "row", 1)
    head_kv = jnp.concatenate(
        [
            lax.dynamic_slice_in_dim(kv_cache, kv_group * head_size, head_size, 1),
            lax.dynamic_slice_in_dim(kv_cache, kv_half + kv_group * head_size, head_size, 1),
        ],
        axis=1,
    )
    attend, initial = make_attend(query_rows, segment, first_row, 0, head_size, head_size)
    running_max, running_sum, running_out = attend(
        initial, ring_gather(head_kv, "col", 0), jnp.int32(0)
    )
    attention = (running_out / running_sum[:, :, None]).astype(jnp.bfloat16)
    attention = jnp.transpose(attention, (1, 0, 2)).reshape(own_rows, query_cols)
    return (attention, kv_cache)


def solution(mesh):
    return jax.shard_map(
        body,
        mesh=mesh,
        in_specs=(
            P(("dp", "row"), "col"),
            P("col", "row"),
            P("col", None),
            P("dp", "col", None),
            P("dp", None, "row"),
            P(),
            P(),
        ),
        out_specs=(P(("dp", "col"), "row"), P(("dp", "col"), None)),
        check_vma=False,
    )
```

```python
import math

import jax
import jax.numpy as jnp
from jax import lax
from jax.sharding import PartitionSpec as P

HEAD_DIM = 128
MOST_LEN = 160


masked_score = -1e30


def block_layout(lengths_row, block_len):
    prefix_len = block_len - jnp.sum(lengths_row)
    ends_at = jnp.cumsum(lengths_row) + prefix_len
    starts = ends_at - lengths_row
    positions = jnp.arange(block_len, dtype=jnp.int32)
    segment = jnp.sum((positions[:, None] >= starts[None, :]).astype(jnp.int32), axis=1)
    return (starts, segment, positions)


def slot_numbers(holders):
    request_total = holders.shape[0]
    ordering = jnp.arange(request_total, dtype=jnp.int32)
    earlier = ordering[None, :] < ordering[:, None]
    same_holder = holders[:, None] == holders[None, :]
    return jnp.sum((earlier & same_holder).astype(jnp.int32), axis=1)


def make_attend(query_rows, segment, first_row, kv_group, head_size, kv_half):
    own_rows = query_rows.shape[0]
    heads_here = query_rows.shape[1] // head_size
    query_heads = query_rows.reshape(own_rows, heads_here, head_size)
    query_pos = first_row + jnp.arange(own_rows, dtype=jnp.int32)
    query_seg = lax.dynamic_slice_in_dim(segment, first_row, own_rows, 0)
    score_scale = 1.0 / math.sqrt(head_size)

    def attend(state_in, key_block, key_start):
        running_max, running_sum, running_out = state_in
        block_size = key_block.shape[0]
        key_rows = lax.dynamic_slice_in_dim(key_block, kv_group * head_size, head_size, 1)
        values = lax.dynamic_slice_in_dim(key_block, kv_half + kv_group * head_size, head_size, 1)
        key_pos = jnp.arange(block_size, dtype=jnp.int32)
        allowed = (key_pos[None, :] <= query_pos[:, None]) & (
            (segment[None, :] == query_seg[:, None]) | (segment[None, :] == 0)
        )
        scores = (
            jnp.einsum("qhd,kd->hqk", query_heads, key_rows, preferred_element_type=jnp.float32)
            * score_scale
        )
        scores = jnp.where(allowed[None], scores, masked_score)
        new_max = jnp.maximum(running_max, jnp.max(scores, axis=2))
        weights = jnp.where(allowed[None], jnp.exp(scores - new_max[:, :, None]), 0.0)
        running_sum = jnp.sum(weights, axis=2)
        running_out = jnp.einsum(
            "hqk,kd->hqd", weights.astype(jnp.bfloat16), values, preferred_element_type=jnp.float32
        )
        return (new_max, running_sum, running_out)

    initial = (
        jnp.full((heads_here, own_rows), masked_score, jnp.float32),
        jnp.zeros((heads_here, own_rows), jnp.float32),
        jnp.zeros((heads_here, own_rows, head_size), jnp.float32),
    )
    return (attend, initial)


def shifted_copies(x, axis_name):
    size = lax.axis_size(axis_name)
    copies = [x]
    for shift in range(1, size):
        perm = [(i, (i - shift) % size) for i in range(size)]
        copies.append(lax.ppermute(x, axis_name, perm))
    return copies


def ring_gather(x, axis_name, axis):
    size = lax.axis_size(axis_name)
    me = lax.axis_index(axis_name)
    copies = shifted_copies(x, axis_name)
    doubled = jnp.stack(copies + copies, axis=0)
    ordered = lax.dynamic_slice_in_dim(doubled, size - me, size, 0)
    moved = jnp.moveaxis(ordered, 0, axis)
    shape = list(x.shape)
    shape[axis] = shape[axis] * size
    return moved.reshape(shape)


def ring_reduce_scatter(x, axis_name):
    size = lax.axis_size(axis_name)
    me = lax.axis_index(axis_name)
    chunk = x.shape[0] // size
    total = lax.dynamic_slice_in_dim(x, me * chunk, chunk, 0)
    for shift in range(1, size):
        perm = [(i, (i + shift) % size) for i in range(size)]
        piece = lax.dynamic_slice_in_dim(x, ((me + shift) % size) * chunk, chunk, 0)
        total = total + lax.ppermute(piece, axis_name, perm)
    return total


def body(hidden_states, w_query, w_key_value, adapter_down, adapter_up, req_lengths, req_adapter):
    dp_size = lax.axis_size("dp")
    block_index = lax.axis_index("dp")
    col_index = lax.axis_index("col")
    row_index = lax.axis_index("row")
    gathered = ring_gather(hidden_states, "row", 0)
    block_len = gathered.shape[0]
    query_cols = w_query.shape[1]
    kv_cols = w_key_value.shape[1]
    kv_half = kv_cols // 2
    head_size = HEAD_DIM
    heads_here = query_cols // head_size
    heads_total = heads_here * lax.axis_size("row")
    kv_heads = kv_half // head_size
    kv_group = row_index * heads_here // (heads_total // kv_heads)
    own_rows = block_len // lax.axis_size("col")
    first_row = col_index * own_rows
    held_sets = adapter_down.shape[0]
    width_here = adapter_down.shape[1]
    rank_size = adapter_down.shape[2]
    lengths_row = req_lengths[block_index]
    adapters_row = req_adapter[block_index]
    requests = lengths_row.shape[0]
    starts, segment, positions = block_layout(lengths_row, block_len)
    request_of = jnp.clip(segment - 1, 0, requests - 1)
    in_request = segment > 0
    holders = adapters_row // held_sets
    wanted_from_me = (req_adapter // held_sets) == block_index
    local_pick = jnp.sum(jnp.where(wanted_from_me, req_adapter % held_sets, 0), axis=1)
    down_pick = jnp.transpose(jnp.take(adapter_down, local_pick, axis=0), (0, 2, 1))
    up_pick = jnp.take(adapter_up, local_pick, axis=0)
    outgoing = jnp.concatenate([down_pick, up_pick], axis=1)
    incoming = lax.all_to_all(outgoing, "dp", split_axis=0, concat_axis=0, tiled=True)
    flat_down = incoming[:, :rank_size, :].reshape(dp_size * rank_size, width_here).T
    flat_up = incoming[:, rank_size:, :].reshape(dp_size * rank_size, query_cols).astype(jnp.float32)
    reduced = jnp.dot(gathered, flat_down, preferred_element_type=jnp.float32)
    request_ids = jnp.arange(requests, dtype=jnp.int32)
    token_holder = jnp.sum(
        jnp.where(segment[:, None] == request_ids[None, :] + 1, holders[None, :] + 1, 0), axis=1
    ) - 1
    slot_ids = jnp.arange(dp_size, dtype=jnp.int32)
    token_mask = slot_ids[None, :] == token_holder[:, None]
    reduced = reduced.reshape(block_len, dp_size, rank_size)
    low_partial = jnp.sum(jnp.where(token_mask[:, :, None], reduced, 0.0), axis=1)
    low_rank = ring_reduce_scatter(low_partial, "col")
    own_mask = lax.dynamic_slice_in_dim(token_mask, first_row, own_rows, 0)
    spread = jnp.where(own_mask[:, :, None], low_rank[:, None, :], 0.0)
    spread = spread.reshape(own_rows, dp_size * rank_size)
    adapter_term = jnp.dot(spread, flat_up, precision=lax.Precision.HIGHEST)
    key_cols = lax.dynamic_slice_in_dim(w_key_value, kv_group * head_size, head_size, 1)
    value_cols = lax.dynamic_slice_in_dim(w_key_value, kv_half + kv_group * head_size, head_size, 1)
    both_weights = jnp.concatenate([w_query, key_cols, value_cols], axis=1)
    partial_value = jnp.dot(gathered, both_weights, preferred_element_type=jnp.float32)
    summed = ring_reduce_scatter(partial_value, "col")
    query_rows = (summed[:, :query_cols] + adapter_term).astype(jnp.bfloat16)
    head_kv = summed[:, query_cols:].astype(jnp.bfloat16)
    row_size = lax.axis_size("row")
    partner = [(i, (i + row_size // kv_heads) % row_size) for i in range(row_size)]
    other_kv = lax.ppermute(head_kv, "row", partner)
    first_is_own = kv_group == 0
    low_head = jnp.where(first_is_own, head_kv, other_kv)
    high_head = jnp.where(first_is_own, other_kv, head_kv)
    kv_cache = jnp.concatenate(
        [low_head[:, :head_size], high_head[:, :head_size], low_head[:, head_size:], high_head[:, head_size:]],
        axis=1,
    )
    attend, initial = make_attend(query_rows, segment, first_row, 0, head_size, head_size)
    running_max, running_sum, running_out = attend(
        initial, ring_gather(head_kv, "col", 0), jnp.int32(0)
    )
    attention = (running_out / running_sum[:, :, None]).astype(jnp.bfloat16)
    attention = jnp.transpose(attention, (1, 0, 2)).reshape(own_rows, query_cols)
    return (attention, kv_cache)


def solution(mesh):
    return jax.shard_map(
        body,
        mesh=mesh,
        in_specs=(
            P(("dp", "row"), "col"),
            P("col", "row"),
            P("col", None),
            P("dp", "col", None),
            P("dp", None, "row"),
            P(),
            P(),
        ),
        out_specs=(P(("dp", "col"), "row"), P(("dp", "col"), None)),
        check_vma=False,
    )
```

```python
import math

import jax
import jax.numpy as jnp
from jax import lax
from jax.sharding import PartitionSpec as P


HEAD_DIM = 128


masked_score = -1e30


def block_layout(lengths_row, block_len):
    prefix_len = block_len - jnp.sum(lengths_row)
    ends_at = jnp.cumsum(lengths_row) + prefix_len
    starts = ends_at - lengths_row
    positions = jnp.arange(block_len, dtype=jnp.int32)
    segment = jnp.sum((positions[:, None] >= starts[None, :]).astype(jnp.int32), axis=1)
    return (starts, segment, positions)


def make_attend(query_rows, segment, first_row, kv_group, head_size, kv_half):
    own_rows = query_rows.shape[0]
    heads_here = query_rows.shape[1] // head_size
    query_heads = query_rows.reshape(own_rows, heads_here, head_size)
    query_pos = first_row + jnp.arange(own_rows, dtype=jnp.int32)
    query_seg = lax.dynamic_slice_in_dim(segment, first_row, own_rows, 0)
    score_scale = 1.0 / math.sqrt(head_size)

    def attend(state_in, key_block, key_start):
        running_max, running_sum, running_out = state_in
        block_size = key_block.shape[0]
        key_rows = lax.dynamic_slice_in_dim(key_block, kv_group * head_size, head_size, 1)
        values = lax.dynamic_slice_in_dim(key_block, kv_half + kv_group * head_size, head_size, 1)
        key_pos = jnp.arange(block_size, dtype=jnp.int32)
        allowed = (key_pos[None, :] <= query_pos[:, None]) & (
            (segment[None, :] == query_seg[:, None]) | (segment[None, :] == 0)
        )
        scores = (
            jnp.einsum("qhd,kd->hqk", query_heads, key_rows, preferred_element_type=jnp.float32)
            * score_scale
        )
        scores = jnp.where(allowed[None], scores, masked_score)
        new_max = jnp.maximum(running_max, jnp.max(scores, axis=2))
        weights = jnp.where(allowed[None], jnp.exp(scores - new_max[:, :, None]), 0.0)
        running_sum = jnp.sum(weights, axis=2)
        running_out = jnp.einsum(
            "hqk,kd->hqd", weights.astype(jnp.bfloat16), values, preferred_element_type=jnp.float32
        )
        return (new_max, running_sum, running_out)

    initial = (
        jnp.full((heads_here, own_rows), masked_score, jnp.float32),
        jnp.zeros((heads_here, own_rows), jnp.float32),
        jnp.zeros((heads_here, own_rows, head_size), jnp.float32),
    )
    return (attend, initial)


def shifted_copies(x, axis_name):
    size = lax.axis_size(axis_name)
    copies = [x]
    for shift in range(1, size):
        perm = [(i, (i - shift) % size) for i in range(size)]
        copies.append(lax.ppermute(x, axis_name, perm))
    return copies


def ring_gather(x, axis_name, axis):
    size = lax.axis_size(axis_name)
    me = lax.axis_index(axis_name)
    copies = shifted_copies(x, axis_name)
    doubled = jnp.stack(copies + copies, axis=0)
    ordered = lax.dynamic_slice_in_dim(doubled, size - me, size, 0)
    moved = jnp.moveaxis(ordered, 0, axis)
    shape = list(x.shape)
    shape[axis] = shape[axis] * size
    return moved.reshape(shape)


def ring_reduce_scatter(x, axis_name):
    size = lax.axis_size(axis_name)
    me = lax.axis_index(axis_name)
    chunk = x.shape[0] // size
    total = lax.dynamic_slice_in_dim(x, me * chunk, chunk, 0)
    for shift in range(1, size):
        perm = [(i, (i + shift) % size) for i in range(size)]
        piece = lax.dynamic_slice_in_dim(x, ((me + shift) % size) * chunk, chunk, 0)
        total = total + lax.ppermute(piece, axis_name, perm)
    return total


def col_exchange(partial, shared):
    size = lax.axis_size("col")
    me = lax.axis_index("col")
    chunk = partial.shape[0] // size
    width = partial.shape[1]
    total = lax.dynamic_slice_in_dim(partial, me * chunk, chunk, 0)
    copies = [shared]
    wide = shared.astype(partial.dtype)
    for shift in range(1, size):
        perm = [(i, (i + shift) % size) for i in range(size)]
        piece = lax.dynamic_slice_in_dim(partial, ((me + shift) % size) * chunk, chunk, 0)
        got = lax.ppermute(jnp.concatenate([piece, wide], axis=1), "col", perm)
        total = total + got[:, :width]
        copies.append(got[:, width:].astype(shared.dtype))
    doubled = jnp.stack(copies + copies, axis=0)[::-1]
    ordered = lax.dynamic_slice_in_dim(doubled, size - 1 - me, size, 0)
    return total, ordered.reshape((size * shared.shape[0],) + shared.shape[1:])


def body(hidden_states, w_query, w_key_value, adapter_down, adapter_up, req_lengths, req_adapter):
    dp_size = lax.axis_size("dp")
    block_index = lax.axis_index("dp")
    col_index = lax.axis_index("col")
    row_index = lax.axis_index("row")
    gathered = ring_gather(hidden_states, "row", 0)
    block_len = gathered.shape[0]
    query_cols = w_query.shape[1]
    kv_cols = w_key_value.shape[1]
    kv_half = kv_cols // 2
    head_size = HEAD_DIM
    heads_here = query_cols // head_size
    heads_total = heads_here * lax.axis_size("row")
    kv_heads = kv_half // head_size
    kv_group = row_index * heads_here // (heads_total // kv_heads)
    own_rows = block_len // lax.axis_size("col")
    first_row = col_index * own_rows
    held_sets = adapter_down.shape[0]
    width_here = adapter_down.shape[1]
    rank_size = adapter_down.shape[2]
    lengths_row = req_lengths[block_index]
    adapters_row = req_adapter[block_index]
    requests = lengths_row.shape[0]
    _, segment, _ = block_layout(lengths_row, block_len)
    request_of = jnp.clip(segment - 1, 0, requests - 1)
    holders = adapters_row // held_sets
    wanted_from_me = (req_adapter // held_sets) == block_index
    local_pick = jnp.sum(jnp.where(wanted_from_me, req_adapter % held_sets, 0), axis=1)
    down_pick = jnp.transpose(jnp.take(adapter_down, local_pick, axis=0), (0, 2, 1))
    up_pick = jnp.take(adapter_up, local_pick, axis=0)
    outgoing = jnp.concatenate([down_pick, up_pick], axis=1)
    incoming = lax.all_to_all(outgoing, "dp", split_axis=0, concat_axis=0, tiled=True)
    flat_down = incoming[:, :rank_size, :].reshape(dp_size * rank_size, width_here).T
    flat_up = incoming[:, rank_size:, :].reshape(dp_size * rank_size, query_cols).astype(jnp.float32)
    reduced = jnp.dot(gathered, flat_down, preferred_element_type=jnp.float32)
    request_ids = jnp.arange(requests, dtype=jnp.int32)
    token_holder = jnp.sum(
        jnp.where(segment[:, None] == request_ids[None, :] + 1, holders[None, :] + 1, 0), axis=1
    ) - 1
    slot_ids = jnp.arange(dp_size, dtype=jnp.int32)
    token_mask = slot_ids[None, :] == token_holder[:, None]
    reduced = reduced.reshape(block_len, dp_size, rank_size)
    low_partial = jnp.sum(jnp.where(token_mask[:, :, None], reduced, 0.0), axis=1)
    key_cols = lax.dynamic_slice_in_dim(w_key_value, kv_group * head_size, head_size, 1)
    value_cols = lax.dynamic_slice_in_dim(w_key_value, kv_half + kv_group * head_size, head_size, 1)
    both_weights = jnp.concatenate([w_query, key_cols, value_cols], axis=1)
    partial_value = jnp.dot(gathered, both_weights, preferred_element_type=jnp.float32)
    summed = ring_reduce_scatter(partial_value, "col")
    head_kv = summed[:, query_cols:].astype(jnp.bfloat16)
    low_rank, key_values = col_exchange(low_partial, head_kv)
    own_mask = lax.dynamic_slice_in_dim(token_mask, first_row, own_rows, 0)
    spread = jnp.where(own_mask[:, :, None], low_rank[:, None, :], 0.0)
    spread = spread.reshape(own_rows, dp_size * rank_size)
    adapter_term = jnp.dot(spread, flat_up, precision=lax.Precision.HIGHEST)
    query_rows = (summed[:, :query_cols] + adapter_term).astype(jnp.bfloat16)
    row_size = lax.axis_size("row")
    partner = [(i, (i + row_size // kv_heads) % row_size) for i in range(row_size)]
    other_kv = lax.ppermute(head_kv, "row", partner)
    first_is_own = kv_group == 0
    low_head = jnp.where(first_is_own, head_kv, other_kv)
    high_head = jnp.where(first_is_own, other_kv, head_kv)
    kv_cache = jnp.concatenate(
        [low_head[:, :head_size], high_head[:, :head_size], low_head[:, head_size:], high_head[:, head_size:]],
        axis=1,
    )
    attend, initial = make_attend(query_rows, segment, first_row, 0, head_size, head_size)
    _, running_sum, running_out = attend(
        initial, key_values, jnp.int32(0)
    )
    attention = (running_out / running_sum[:, :, None]).astype(jnp.bfloat16)
    attention = jnp.transpose(attention, (1, 0, 2)).reshape(own_rows, query_cols)
    return (attention, kv_cache)


def solution(mesh):
    return jax.shard_map(
        body,
        mesh=mesh,
        in_specs=(
            P(("dp", "row"), "col"),
            P("col", "row"),
            P("col", None),
            P("dp", "col", None),
            P("dp", None, "row"),
            P(),
            P(),
        ),
        out_specs=(P(("dp", "col"), "row"), P(("dp", "col"), None)),
        check_vma=False,
    )
```

```python
import math

import jax
import jax.numpy as jnp
from jax import lax
from jax.sharding import PartitionSpec as P


HEAD_DIM = 128


masked_score = -1e30


def block_layout(lengths_row, block_len):
    prefix_len = block_len - jnp.sum(lengths_row)
    ends_at = jnp.cumsum(lengths_row) + prefix_len
    starts = ends_at - lengths_row
    positions = jnp.arange(block_len, dtype=jnp.int32)
    segment = jnp.sum((positions[:, None] >= starts[None, :]).astype(jnp.int32), axis=1)
    return (starts, segment, positions)


def make_attend(query_rows, segment, first_row, kv_group, head_size, kv_half):
    own_rows = query_rows.shape[0]
    heads_here = query_rows.shape[1] // head_size
    query_heads = query_rows.reshape(own_rows, heads_here, head_size)
    query_pos = first_row + jnp.arange(own_rows, dtype=jnp.int32)
    query_seg = lax.dynamic_slice_in_dim(segment, first_row, own_rows, 0)
    score_scale = 1.0 / math.sqrt(head_size)

    def attend(state_in, key_block, key_start):
        running_max, running_sum, running_out = state_in
        block_size = key_block.shape[0]
        key_rows = lax.dynamic_slice_in_dim(key_block, kv_group * head_size, head_size, 1)
        values = lax.dynamic_slice_in_dim(key_block, kv_half + kv_group * head_size, head_size, 1)
        key_pos = jnp.arange(block_size, dtype=jnp.int32)
        allowed = (key_pos[None, :] <= query_pos[:, None]) & (
            (segment[None, :] == query_seg[:, None]) | (segment[None, :] == 0)
        )
        scores = (
            jnp.einsum("qhd,kd->hqk", query_heads, key_rows, preferred_element_type=jnp.float32)
            * score_scale
        )
        scores = jnp.where(allowed[None], scores, masked_score)
        new_max = jnp.maximum(running_max, jnp.max(scores, axis=2))
        weights = jnp.where(allowed[None], jnp.exp(scores - new_max[:, :, None]), 0.0)
        running_sum = jnp.sum(weights, axis=2)
        running_out = jnp.einsum(
            "hqk,kd->hqd", weights.astype(jnp.bfloat16), values, preferred_element_type=jnp.float32
        )
        return (new_max, running_sum, running_out)

    initial = (
        jnp.full((heads_here, own_rows), masked_score, jnp.float32),
        jnp.zeros((heads_here, own_rows), jnp.float32),
        jnp.zeros((heads_here, own_rows, head_size), jnp.float32),
    )
    return (attend, initial)


def shifted_copies(x, axis_name):
    size = lax.axis_size(axis_name)
    copies = [x]
    for shift in range(1, size):
        perm = [(i, (i - shift) % size) for i in range(size)]
        copies.append(lax.ppermute(x, axis_name, perm))
    return copies


def ring_gather(x, axis_name, axis):
    size = lax.axis_size(axis_name)
    me = lax.axis_index(axis_name)
    copies = shifted_copies(x, axis_name)
    doubled = jnp.stack(copies + copies, axis=0)
    ordered = lax.dynamic_slice_in_dim(doubled, size - me, size, 0)
    moved = jnp.moveaxis(ordered, 0, axis)
    shape = list(x.shape)
    shape[axis] = shape[axis] * size
    return moved.reshape(shape)


def ring_reduce_scatter(x, axis_name):
    size = lax.axis_size(axis_name)
    me = lax.axis_index(axis_name)
    chunk = x.shape[0] // size
    total = lax.dynamic_slice_in_dim(x, me * chunk, chunk, 0)
    for shift in range(1, size):
        perm = [(i, (i + shift) % size) for i in range(size)]
        piece = lax.dynamic_slice_in_dim(x, ((me + shift) % size) * chunk, chunk, 0)
        total = total + lax.ppermute(piece, axis_name, perm)
    return total


def body(hidden_states, w_query, w_key_value, adapter_down, adapter_up, req_lengths, req_adapter):
    dp_size = lax.axis_size("dp")
    block_index = lax.axis_index("dp")
    col_index = lax.axis_index("col")
    row_index = lax.axis_index("row")
    gathered = ring_gather(hidden_states, "row", 0)
    block_len = gathered.shape[0]
    query_cols = w_query.shape[1]
    kv_cols = w_key_value.shape[1]
    kv_half = kv_cols // 2
    head_size = HEAD_DIM
    heads_here = query_cols // head_size
    heads_total = heads_here * lax.axis_size("row")
    kv_heads = kv_half // head_size
    kv_group = row_index * heads_here // (heads_total // kv_heads)
    own_rows = block_len // lax.axis_size("col")
    first_row = col_index * own_rows
    held_sets = adapter_down.shape[0]
    width_here = adapter_down.shape[1]
    rank_size = adapter_down.shape[2]
    lengths_row = req_lengths[block_index]
    adapters_row = req_adapter[block_index]
    requests = lengths_row.shape[0]
    _, segment, _ = block_layout(lengths_row, block_len)
    request_of = jnp.clip(segment - 1, 0, requests - 1)
    holders = adapters_row // held_sets
    wanted_from_me = (req_adapter // held_sets) == block_index
    local_pick = jnp.sum(jnp.where(wanted_from_me, req_adapter % held_sets, 0), axis=1)
    down_pick = jnp.transpose(jnp.take(adapter_down, local_pick, axis=0), (0, 2, 1))
    up_pick = jnp.take(adapter_up, local_pick, axis=0)
    outgoing = jnp.concatenate([down_pick, up_pick], axis=1)
    incoming = lax.all_to_all(outgoing, "dp", split_axis=0, concat_axis=0, tiled=True)
    flat_down = incoming[:, :rank_size, :].reshape(dp_size * rank_size, width_here).T
    flat_up = incoming[:, rank_size:, :].reshape(dp_size * rank_size, query_cols).astype(jnp.float32)
    reduced = jnp.dot(gathered, flat_down, preferred_element_type=jnp.float32)
    request_ids = jnp.arange(requests, dtype=jnp.int32)
    token_holder = jnp.sum(
        jnp.where(segment[:, None] == request_ids[None, :] + 1, holders[None, :] + 1, 0), axis=1
    ) - 1
    slot_ids = jnp.arange(dp_size, dtype=jnp.int32)
    token_mask = slot_ids[None, :] == token_holder[:, None]
    reduced = reduced.reshape(block_len, dp_size, rank_size)
    kept = jnp.where(token_mask[:, :, None], reduced, 0.0).reshape(block_len, dp_size * rank_size)
    adapter_part = jnp.dot(kept, flat_up, precision=lax.Precision.HIGHEST)
    key_cols = lax.dynamic_slice_in_dim(w_key_value, kv_group * head_size, head_size, 1)
    value_cols = lax.dynamic_slice_in_dim(w_key_value, kv_half + kv_group * head_size, head_size, 1)
    head_weights = jnp.concatenate([key_cols, value_cols], axis=1)
    partial_kv = jnp.dot(gathered, head_weights, preferred_element_type=jnp.float32)
    head_kv = ring_reduce_scatter(partial_kv, "col").astype(jnp.bfloat16)
    partial_query = jnp.dot(gathered, w_query, preferred_element_type=jnp.float32) + adapter_part
    query_rows = ring_reduce_scatter(partial_query, "col").astype(jnp.bfloat16)
    row_size = lax.axis_size("row")
    partner = [(i, (i + row_size // kv_heads) % row_size) for i in range(row_size)]
    other_kv = lax.ppermute(head_kv, "row", partner)
    key_values = ring_gather(head_kv, "col", 0)
    first_is_own = kv_group == 0
    low_head = jnp.where(first_is_own, head_kv, other_kv)
    high_head = jnp.where(first_is_own, other_kv, head_kv)
    kv_cache = jnp.concatenate(
        [low_head[:, :head_size], high_head[:, :head_size], low_head[:, head_size:], high_head[:, head_size:]],
        axis=1,
    )
    attend, initial = make_attend(query_rows, segment, first_row, 0, head_size, head_size)
    _, running_sum, running_out = attend(
        initial, key_values, jnp.int32(0)
    )
    attention = (running_out / running_sum[:, :, None]).astype(jnp.bfloat16)
    attention = jnp.transpose(attention, (1, 0, 2)).reshape(own_rows, query_cols)
    return (attention, kv_cache)


def solution(mesh):
    return jax.shard_map(
        body,
        mesh=mesh,
        in_specs=(
            P(("dp", "row"), "col"),
            P("col", "row"),
            P("col", None),
            P("dp", "col", None),
            P("dp", None, "row"),
            P(),
            P(),
        ),
        out_specs=(P(("dp", "col"), "row"), P(("dp", "col"), None)),
        check_vma=False,
    )
```

```python
import math

import jax
import jax.numpy as jnp
from jax import lax
from jax.sharding import PartitionSpec as P


HEAD_DIM = 128


masked_score = -1e30


def block_layout(lengths_row, block_len):
    prefix_len = block_len - jnp.sum(lengths_row)
    ends_at = jnp.cumsum(lengths_row) + prefix_len
    starts = ends_at - lengths_row
    positions = jnp.arange(block_len, dtype=jnp.int32)
    segment = jnp.sum((positions[:, None] >= starts[None, :]).astype(jnp.int32), axis=1)
    return (starts, segment, positions)


def make_attend(query_rows, segment, first_row, kv_group, head_size, kv_half):
    own_rows = query_rows.shape[0]
    heads_here = query_rows.shape[1] // head_size
    query_heads = query_rows.reshape(own_rows, heads_here, head_size)
    query_pos = first_row + jnp.arange(own_rows, dtype=jnp.int32)
    query_seg = lax.dynamic_slice_in_dim(segment, first_row, own_rows, 0)
    score_scale = 1.0 / math.sqrt(head_size)

    def attend(state_in, key_block, key_start):
        running_max, running_sum, running_out = state_in
        block_size = key_block.shape[0]
        key_rows = lax.dynamic_slice_in_dim(key_block, kv_group * head_size, head_size, 1)
        values = lax.dynamic_slice_in_dim(key_block, kv_half + kv_group * head_size, head_size, 1)
        key_pos = jnp.arange(block_size, dtype=jnp.int32)
        allowed = (key_pos[None, :] <= query_pos[:, None]) & (
            (segment[None, :] == query_seg[:, None]) | (segment[None, :] == 0)
        )
        scores = (
            jnp.einsum("qhd,kd->hqk", query_heads, key_rows, preferred_element_type=jnp.float32)
            * score_scale
        )
        scores = jnp.where(allowed[None], scores, masked_score)
        new_max = jnp.maximum(running_max, jnp.max(scores, axis=2))
        weights = jnp.where(allowed[None], jnp.exp(scores - new_max[:, :, None]), 0.0)
        running_sum = jnp.sum(weights, axis=2)
        running_out = jnp.einsum(
            "hqk,kd->hqd", weights.astype(jnp.bfloat16), values, preferred_element_type=jnp.float32
        )
        return (new_max, running_sum, running_out)

    initial = (
        jnp.full((heads_here, own_rows), masked_score, jnp.float32),
        jnp.zeros((heads_here, own_rows), jnp.float32),
        jnp.zeros((heads_here, own_rows, head_size), jnp.float32),
    )
    return (attend, initial)


def shifted_copies(x, axis_name):
    size = lax.axis_size(axis_name)
    copies = [x]
    for shift in range(1, size):
        perm = [(i, (i - shift) % size) for i in range(size)]
        copies.append(lax.ppermute(x, axis_name, perm))
    return copies


def ring_gather(x, axis_name, axis):
    size = lax.axis_size(axis_name)
    me = lax.axis_index(axis_name)
    copies = shifted_copies(x, axis_name)
    doubled = jnp.stack(copies + copies, axis=0)
    ordered = lax.dynamic_slice_in_dim(doubled, size - me, size, 0)
    moved = jnp.moveaxis(ordered, 0, axis)
    shape = list(x.shape)
    shape[axis] = shape[axis] * size
    return moved.reshape(shape)


def ring_reduce_scatter(x, axis_name):
    size = lax.axis_size(axis_name)
    me = lax.axis_index(axis_name)
    chunk = x.shape[0] // size
    total = lax.dynamic_slice_in_dim(x, me * chunk, chunk, 0)
    for shift in range(1, size):
        perm = [(i, (i + shift) % size) for i in range(size)]
        piece = lax.dynamic_slice_in_dim(x, ((me + shift) % size) * chunk, chunk, 0)
        total = total + lax.ppermute(piece, axis_name, perm)
    return total


def body(hidden_states, w_query, w_key_value, adapter_down, adapter_up, req_lengths, req_adapter):
    dp_size = lax.axis_size("dp")
    block_index = lax.axis_index("dp")
    col_index = lax.axis_index("col")
    row_index = lax.axis_index("row")
    gathered = ring_gather(hidden_states, "row", 0)
    block_len = gathered.shape[0]
    query_cols = w_query.shape[1]
    kv_cols = w_key_value.shape[1]
    kv_half = kv_cols // 2
    head_size = HEAD_DIM
    heads_here = query_cols // head_size
    heads_total = heads_here * lax.axis_size("row")
    kv_heads = kv_half // head_size
    kv_group = row_index * heads_here // (heads_total // kv_heads)
    own_rows = block_len // lax.axis_size("col")
    first_row = col_index * own_rows
    held_sets = adapter_down.shape[0]
    width_here = adapter_down.shape[1]
    rank_size = adapter_down.shape[2]
    lengths_row = req_lengths[block_index]
    adapters_row = req_adapter[block_index]
    requests = lengths_row.shape[0]
    _, segment, _ = block_layout(lengths_row, block_len)
    request_of = jnp.clip(segment - 1, 0, requests - 1)
    holders = adapters_row // held_sets
    wanted_from_me = (req_adapter // held_sets) == block_index
    local_pick = jnp.sum(jnp.where(wanted_from_me, req_adapter % held_sets, 0), axis=1)
    down_pick = jnp.transpose(jnp.take(adapter_down, local_pick, axis=0), (0, 2, 1))
    up_pick = jnp.take(adapter_up, local_pick, axis=0)
    outgoing = jnp.concatenate([down_pick, up_pick], axis=1)
    incoming = lax.all_to_all(outgoing, "dp", split_axis=0, concat_axis=0, tiled=True)
    flat_down = incoming[:, :rank_size, :].reshape(dp_size * rank_size, width_here).T
    flat_up = incoming[:, rank_size:, :].reshape(dp_size * rank_size, query_cols).astype(jnp.float32)
    reduced = jnp.dot(gathered, flat_down, preferred_element_type=jnp.float32)
    request_ids = jnp.arange(requests, dtype=jnp.int32)
    token_holder = jnp.sum(
        jnp.where(segment[:, None] == request_ids[None, :] + 1, holders[None, :] + 1, 0), axis=1
    ) - 1
    slot_ids = jnp.arange(dp_size, dtype=jnp.int32)
    token_mask = slot_ids[None, :] == token_holder[:, None]
    reduced = reduced.reshape(block_len, dp_size, rank_size)
    low_partial = jnp.sum(jnp.where(token_mask[:, :, None], reduced, 0.0), axis=1)
    low_rank = ring_reduce_scatter(low_partial, "col")
    own_mask = lax.dynamic_slice_in_dim(token_mask, first_row, own_rows, 0)
    spread = jnp.where(own_mask[:, :, None], low_rank[:, None, :], 0.0)
    spread = spread.reshape(own_rows, dp_size * rank_size)
    adapter_term = jnp.dot(spread, flat_up, precision=lax.Precision.HIGHEST)
    key_cols = lax.dynamic_slice_in_dim(w_key_value, kv_group * head_size, head_size, 1)
    value_cols = lax.dynamic_slice_in_dim(w_key_value, kv_half + kv_group * head_size, head_size, 1)
    both_weights = jnp.concatenate([w_query, key_cols, value_cols], axis=1)
    partial_value = jnp.dot(gathered, both_weights, preferred_element_type=jnp.float32)
    summed = ring_reduce_scatter(partial_value, "col")
    query_rows = (summed[:, :query_cols] + adapter_term).astype(jnp.bfloat16)
    head_kv = summed[:, query_cols:].astype(jnp.bfloat16)
    row_size = lax.axis_size("row")
    partner = [(i, (i + row_size // kv_heads) % row_size) for i in range(row_size)]
    other_kv = lax.ppermute(head_kv, "row", partner)
    first_is_own = kv_group == 0
    low_head = jnp.where(first_is_own, head_kv, other_kv)
    high_head = jnp.where(first_is_own, other_kv, head_kv)
    kv_cache = jnp.concatenate(
        [low_head[:, :head_size], high_head[:, :head_size], low_head[:, head_size:], high_head[:, head_size:]],
        axis=1,
    )
    attend, initial = make_attend(query_rows, segment, first_row, 0, head_size, head_size)
    _, running_sum, running_out = attend(initial, ring_gather(head_kv, "col", 0), jnp.int32(0))
    attention = (running_out / running_sum[:, :, None]).astype(jnp.bfloat16)
    attention = jnp.transpose(attention, (1, 0, 2)).reshape(own_rows, query_cols)
    return (attention, kv_cache)


def solution(mesh):
    return jax.shard_map(
        body,
        mesh=mesh,
        in_specs=(
            P(("dp", "row"), "col"),
            P("col", "row"),
            P("col", None),
            P("dp", "col", None),
            P("dp", None, "row"),
            P(),
            P(),
        ),
        out_specs=(P(("dp", "col"), "row"), P(("dp", "col"), None)),
        check_vma=False,
    )
```

```python
import math

import jax
import jax.numpy as jnp
from jax import lax
from jax.sharding import PartitionSpec as P


HEAD_DIM = 128


masked_score = -1e30


def block_layout(lengths_row, block_len):
    prefix_len = block_len - jnp.sum(lengths_row)
    ends_at = jnp.cumsum(lengths_row) + prefix_len
    starts = ends_at - lengths_row
    positions = jnp.arange(block_len, dtype=jnp.int32)
    segment = jnp.sum((positions[:, None] >= starts[None, :]).astype(jnp.int32), axis=1)
    return (starts, segment, positions)


def make_attend(query_rows, segment, first_row, kv_group, head_size, kv_half):
    own_rows = query_rows.shape[0]
    heads_here = query_rows.shape[1] // head_size
    query_heads = query_rows.reshape(own_rows, heads_here, head_size)
    query_pos = first_row + jnp.arange(own_rows, dtype=jnp.int32)
    query_seg = lax.dynamic_slice_in_dim(segment, first_row, own_rows, 0)
    score_scale = 1.0 / math.sqrt(head_size)

    def attend(state_in, key_block, key_start):
        running_max, running_sum, running_out = state_in
        block_size = key_block.shape[0]
        key_rows = lax.dynamic_slice_in_dim(key_block, kv_group * head_size, head_size, 1)
        values = lax.dynamic_slice_in_dim(key_block, kv_half + kv_group * head_size, head_size, 1)
        parts = block_size // own_rows
        blocks = jnp.arange(block_size, dtype=jnp.int32).reshape(parts, own_rows)
        blocks = jnp.concatenate([blocks, blocks], axis=0)
        key_pos = lax.dynamic_slice_in_dim(blocks, key_start, parts, 0).reshape(-1)
        seg_blocks = segment.reshape(parts, own_rows)
        seg_blocks = jnp.concatenate([seg_blocks, seg_blocks], axis=0)
        key_seg = lax.dynamic_slice_in_dim(seg_blocks, key_start, parts, 0).reshape(-1)
        allowed = (key_pos[None, :] <= query_pos[:, None]) & (
            (key_seg[None, :] == query_seg[:, None]) | (key_seg[None, :] == 0)
        )
        scores = (
            jnp.einsum("qhd,kd->hqk", query_heads, key_rows, preferred_element_type=jnp.float32)
            * score_scale
        )
        scores = jnp.where(allowed[None], scores, masked_score)
        new_max = jnp.maximum(running_max, jnp.max(scores, axis=2))
        weights = jnp.where(allowed[None], jnp.exp(scores - new_max[:, :, None]), 0.0)
        running_sum = jnp.sum(weights, axis=2)
        running_out = jnp.einsum(
            "hqk,kd->hqd", weights.astype(jnp.bfloat16), values, preferred_element_type=jnp.float32
        )
        return (new_max, running_sum, running_out)

    initial = (
        jnp.full((heads_here, own_rows), masked_score, jnp.float32),
        jnp.zeros((heads_here, own_rows), jnp.float32),
        jnp.zeros((heads_here, own_rows, head_size), jnp.float32),
    )
    return (attend, initial)


def shifted_copies(x, axis_name):
    size = lax.axis_size(axis_name)
    copies = [x]
    for shift in range(1, size):
        perm = [(i, (i - shift) % size) for i in range(size)]
        copies.append(lax.ppermute(x, axis_name, perm))
    return copies


def ring_reduce_scatter(x, axis_name, origin=0):
    size = lax.axis_size(axis_name)
    me = lax.axis_index(axis_name)
    chunk = x.shape[0] // size
    total = lax.dynamic_slice_in_dim(x, ((me - origin) % size) * chunk, chunk, 0)
    for shift in range(1, size):
        perm = [(i, (i + shift) % size) for i in range(size)]
        piece = lax.dynamic_slice_in_dim(x, ((me + shift - origin) % size) * chunk, chunk, 0)
        total = total + lax.ppermute(piece, axis_name, perm)
    return total


def body(hidden_states, w_query, w_key_value, adapter_down, adapter_up, req_lengths, req_adapter):
    dp_size = lax.axis_size("dp")
    block_index = lax.axis_index("dp")
    col_index = lax.axis_index("col")
    row_index = lax.axis_index("row")
    gathered = jnp.concatenate(shifted_copies(hidden_states, "row"), axis=0)
    block_len = gathered.shape[0]
    query_cols = w_query.shape[1]
    kv_cols = w_key_value.shape[1]
    kv_half = kv_cols // 2
    head_size = HEAD_DIM
    heads_here = query_cols // head_size
    heads_total = heads_here * lax.axis_size("row")
    kv_heads = kv_half // head_size
    kv_group = row_index * heads_here // (heads_total // kv_heads)
    own_rows = block_len // lax.axis_size("col")
    first_row = col_index * own_rows
    held_sets = adapter_down.shape[0]
    width_here = adapter_down.shape[1]
    rank_size = adapter_down.shape[2]
    lengths_row = req_lengths[block_index]
    adapters_row = req_adapter[block_index]
    requests = lengths_row.shape[0]
    _, segment, _ = block_layout(lengths_row, block_len)
    request_of = jnp.clip(segment - 1, 0, requests - 1)
    holders = adapters_row // held_sets
    wanted_from_me = (req_adapter // held_sets) == block_index
    local_pick = jnp.sum(jnp.where(wanted_from_me, req_adapter % held_sets, 0), axis=1)
    down_pick = jnp.transpose(jnp.take(adapter_down, local_pick, axis=0), (0, 2, 1))
    up_pick = jnp.take(adapter_up, local_pick, axis=0)
    outgoing = jnp.concatenate([down_pick, up_pick], axis=1)
    incoming = lax.all_to_all(outgoing, "dp", split_axis=0, concat_axis=0, tiled=True)
    flat_down = incoming[:, :rank_size, :].reshape(dp_size * rank_size, width_here).T
    flat_up = incoming[:, rank_size:, :].reshape(dp_size * rank_size, query_cols).astype(jnp.float32)
    reduced = jnp.dot(gathered, flat_down, preferred_element_type=jnp.float32)
    request_ids = jnp.arange(requests, dtype=jnp.int32)
    token_holder = jnp.sum(
        jnp.where(segment[:, None] == request_ids[None, :] + 1, holders[None, :] + 1, 0), axis=1
    ) - 1
    slot_ids = jnp.arange(dp_size, dtype=jnp.int32)
    token_mask = slot_ids[None, :] == token_holder[:, None]
    row_size = lax.axis_size("row")
    holder_blocks = token_holder.reshape(row_size, -1)
    holder_blocks = jnp.concatenate([holder_blocks, holder_blocks], axis=0)
    gathered_holder = lax.dynamic_slice_in_dim(holder_blocks, row_index, row_size, 0).reshape(-1)
    gathered_mask = slot_ids[None, :] == gathered_holder[:, None]
    reduced = reduced.reshape(block_len, dp_size, rank_size)
    low_partial = jnp.sum(jnp.where(gathered_mask[:, :, None], reduced, 0.0), axis=1)
    low_rank = ring_reduce_scatter(low_partial, "col", row_index)
    own_mask = lax.dynamic_slice_in_dim(token_mask, first_row, own_rows, 0)
    spread = jnp.where(own_mask[:, :, None], low_rank[:, None, :], 0.0)
    spread = spread.reshape(own_rows, dp_size * rank_size)
    adapter_term = jnp.dot(spread, flat_up, precision=lax.Precision.HIGHEST)
    key_cols = lax.dynamic_slice_in_dim(w_key_value, kv_group * head_size, head_size, 1)
    value_cols = lax.dynamic_slice_in_dim(w_key_value, kv_half + kv_group * head_size, head_size, 1)
    both_weights = jnp.concatenate([w_query, key_cols, value_cols], axis=1)
    partial_value = jnp.dot(gathered, both_weights, preferred_element_type=jnp.float32)
    summed = ring_reduce_scatter(partial_value, "col", row_index)
    query_rows = (summed[:, :query_cols] + adapter_term).astype(jnp.bfloat16)
    head_kv = summed[:, query_cols:].astype(jnp.bfloat16)
    partner = [(i, (i + row_size // kv_heads) % row_size) for i in range(row_size)]
    other_kv = lax.ppermute(head_kv, "row", partner)
    key_values = jnp.concatenate(shifted_copies(head_kv, "col"), axis=0)
    first_is_own = kv_group == 0
    low_head = jnp.where(first_is_own, head_kv, other_kv)
    high_head = jnp.where(first_is_own, other_kv, head_kv)
    kv_cache = jnp.concatenate(
        [low_head[:, :head_size], high_head[:, :head_size], low_head[:, head_size:], high_head[:, head_size:]],
        axis=1,
    )
    attend, initial = make_attend(query_rows, segment, first_row, 0, head_size, head_size)
    _, running_sum, running_out = attend(
        initial, key_values, col_index
    )
    attention = (running_out / running_sum[:, :, None]).astype(jnp.bfloat16)
    attention = jnp.transpose(attention, (1, 0, 2)).reshape(own_rows, query_cols)
    return (attention, kv_cache)


def solution(mesh):
    return jax.shard_map(
        body,
        mesh=mesh,
        in_specs=(
            P(("dp", "row"), "col"),
            P("col", "row"),
            P("col", None),
            P("dp", "col", None),
            P("dp", None, "row"),
            P(),
            P(),
        ),
        out_specs=(P(("dp", "col"), "row"), P(("dp", "col"), None)),
        check_vma=False,
    )
```

```python
import math

import jax
import jax.numpy as jnp
from jax import lax
from jax.sharding import PartitionSpec as P


HEAD_DIM = 128


masked_score = -1e30


def block_layout(lengths_row, block_len):
    prefix_len = block_len - jnp.sum(lengths_row)
    ends_at = jnp.cumsum(lengths_row) + prefix_len
    starts = ends_at - lengths_row
    positions = jnp.arange(block_len, dtype=jnp.int32)
    segment = jnp.sum((positions[:, None] >= starts[None, :]).astype(jnp.int32), axis=1)
    return (starts, segment, positions)


def make_attend(query_rows, segment, first_row, kv_group, head_size, kv_half):
    own_rows = query_rows.shape[0]
    heads_here = query_rows.shape[1] // head_size
    query_heads = query_rows.reshape(own_rows, heads_here, head_size)
    query_pos = first_row + jnp.arange(own_rows, dtype=jnp.int32)
    query_seg = lax.dynamic_slice_in_dim(segment, first_row, own_rows, 0)
    score_scale = 1.0 / math.sqrt(head_size)

    def attend(state_in, key_block, key_start):
        running_max, running_sum, running_out = state_in
        block_size = key_block.shape[0]
        key_rows = lax.dynamic_slice_in_dim(key_block, kv_group * head_size, head_size, 1)
        values = lax.dynamic_slice_in_dim(key_block, kv_half + kv_group * head_size, head_size, 1)
        key_pos = jnp.arange(block_size, dtype=jnp.int32)
        allowed = (key_pos[None, :] <= query_pos[:, None]) & (
            (segment[None, :] == query_seg[:, None]) | (segment[None, :] == 0)
        )
        scores = (
            jnp.einsum("qhd,kd->hqk", query_heads, key_rows, preferred_element_type=jnp.float32)
            * score_scale
        )
        scores = jnp.where(allowed[None], scores, masked_score)
        new_max = jnp.maximum(running_max, jnp.max(scores, axis=2))
        weights = jnp.where(allowed[None], jnp.exp(scores - new_max[:, :, None]), 0.0)
        running_sum = jnp.sum(weights, axis=2)
        running_out = jnp.einsum(
            "hqk,kd->hqd", weights.astype(jnp.bfloat16), values, preferred_element_type=jnp.float32
        )
        return (new_max, running_sum, running_out)

    initial = (
        jnp.full((heads_here, own_rows), masked_score, jnp.float32),
        jnp.zeros((heads_here, own_rows), jnp.float32),
        jnp.zeros((heads_here, own_rows, head_size), jnp.float32),
    )
    return (attend, initial)


def shifted_copies(x, axis_name):
    size = lax.axis_size(axis_name)
    copies = [x]
    for shift in range(1, size):
        perm = [(i, (i - shift) % size) for i in range(size)]
        copies.append(lax.ppermute(x, axis_name, perm))
    return copies


def ring_gather(x, axis_name, axis):
    size = lax.axis_size(axis_name)
    me = lax.axis_index(axis_name)
    copies = shifted_copies(x, axis_name)
    doubled = jnp.stack(copies + copies, axis=0)
    ordered = lax.dynamic_slice_in_dim(doubled, size - me, size, 0)
    moved = jnp.moveaxis(ordered, 0, axis)
    shape = list(x.shape)
    shape[axis] = shape[axis] * size
    return moved.reshape(shape)


def ring_reduce_scatter(x, axis_name, origin=0):
    size = lax.axis_size(axis_name)
    me = lax.axis_index(axis_name)
    chunk = x.shape[0] // size
    total = lax.dynamic_slice_in_dim(x, ((me - origin) % size) * chunk, chunk, 0)
    for shift in range(1, size):
        perm = [(i, (i + shift) % size) for i in range(size)]
        piece = lax.dynamic_slice_in_dim(x, ((me + shift - origin) % size) * chunk, chunk, 0)
        total = total + lax.ppermute(piece, axis_name, perm)
    return total


def body(hidden_states, w_query, w_key_value, adapter_down, adapter_up, req_lengths, req_adapter):
    dp_size = lax.axis_size("dp")
    block_index = lax.axis_index("dp")
    col_index = lax.axis_index("col")
    row_index = lax.axis_index("row")
    gathered = jnp.concatenate(shifted_copies(hidden_states, "row"), axis=0)
    block_len = gathered.shape[0]
    query_cols = w_query.shape[1]
    kv_cols = w_key_value.shape[1]
    kv_half = kv_cols // 2
    head_size = HEAD_DIM
    heads_here = query_cols // head_size
    heads_total = heads_here * lax.axis_size("row")
    kv_heads = kv_half // head_size
    kv_group = row_index * heads_here // (heads_total // kv_heads)
    own_rows = block_len // lax.axis_size("col")
    first_row = col_index * own_rows
    held_sets = adapter_down.shape[0]
    width_here = adapter_down.shape[1]
    rank_size = adapter_down.shape[2]
    lengths_row = req_lengths[block_index]
    adapters_row = req_adapter[block_index]
    requests = lengths_row.shape[0]
    _, segment, _ = block_layout(lengths_row, block_len)
    request_of = jnp.clip(segment - 1, 0, requests - 1)
    holders = adapters_row // held_sets
    wanted_from_me = (req_adapter // held_sets) == block_index
    local_pick = jnp.sum(jnp.where(wanted_from_me, req_adapter % held_sets, 0), axis=1)
    down_pick = jnp.transpose(jnp.take(adapter_down, local_pick, axis=0), (0, 2, 1))
    up_pick = jnp.take(adapter_up, local_pick, axis=0)
    outgoing = jnp.concatenate([down_pick, up_pick], axis=1)
    incoming = lax.all_to_all(outgoing, "dp", split_axis=0, concat_axis=0, tiled=True)
    flat_down = incoming[:, :rank_size, :].reshape(dp_size * rank_size, width_here).T
    flat_up = incoming[:, rank_size:, :].reshape(dp_size * rank_size, query_cols).astype(jnp.float32)
    reduced = jnp.dot(gathered, flat_down, preferred_element_type=jnp.float32)
    request_ids = jnp.arange(requests, dtype=jnp.int32)
    token_holder = jnp.sum(
        jnp.where(segment[:, None] == request_ids[None, :] + 1, holders[None, :] + 1, 0), axis=1
    ) - 1
    slot_ids = jnp.arange(dp_size, dtype=jnp.int32)
    token_mask = slot_ids[None, :] == token_holder[:, None]
    row_size = lax.axis_size("row")
    holder_blocks = token_holder.reshape(row_size, -1)
    holder_blocks = jnp.concatenate([holder_blocks, holder_blocks], axis=0)
    gathered_holder = lax.dynamic_slice_in_dim(holder_blocks, row_index, row_size, 0).reshape(-1)
    gathered_mask = slot_ids[None, :] == gathered_holder[:, None]
    reduced = reduced.reshape(block_len, dp_size, rank_size)
    low_partial = jnp.sum(jnp.where(gathered_mask[:, :, None], reduced, 0.0), axis=1)
    low_rank = ring_reduce_scatter(low_partial, "col", row_index)
    own_mask = lax.dynamic_slice_in_dim(token_mask, first_row, own_rows, 0)
    spread = jnp.where(own_mask[:, :, None], low_rank[:, None, :], 0.0)
    spread = spread.reshape(own_rows, dp_size * rank_size)
    adapter_term = jnp.dot(spread, flat_up, precision=lax.Precision.HIGHEST)
    key_cols = lax.dynamic_slice_in_dim(w_key_value, kv_group * head_size, head_size, 1)
    value_cols = lax.dynamic_slice_in_dim(w_key_value, kv_half + kv_group * head_size, head_size, 1)
    both_weights = jnp.concatenate([w_query, key_cols, value_cols], axis=1)
    partial_value = jnp.dot(gathered, both_weights, preferred_element_type=jnp.float32)
    summed = ring_reduce_scatter(partial_value, "col", row_index)
    query_rows = (summed[:, :query_cols] + adapter_term).astype(jnp.bfloat16)
    head_kv = summed[:, query_cols:].astype(jnp.bfloat16)
    partner = [(i, (i + row_size // kv_heads) % row_size) for i in range(row_size)]
    key_values = ring_gather(head_kv, "col", 0)
    other_kv = lax.ppermute(head_kv, "row", partner)
    first_is_own = kv_group == 0
    low_head = jnp.where(first_is_own, head_kv, other_kv)
    high_head = jnp.where(first_is_own, other_kv, head_kv)
    kv_cache = jnp.concatenate(
        [low_head[:, :head_size], high_head[:, :head_size], low_head[:, head_size:], high_head[:, head_size:]],
        axis=1,
    )
    attend, initial = make_attend(query_rows, segment, first_row, 0, head_size, head_size)
    _, running_sum, running_out = attend(
        initial, key_values, jnp.int32(0)
    )
    attention = (running_out / running_sum[:, :, None]).astype(jnp.bfloat16)
    attention = jnp.transpose(attention, (1, 0, 2)).reshape(own_rows, query_cols)
    return (attention, kv_cache)


def solution(mesh):
    return jax.shard_map(
        body,
        mesh=mesh,
        in_specs=(
            P(("dp", "row"), "col"),
            P("col", "row"),
            P("col", None),
            P("dp", "col", None),
            P("dp", None, "row"),
            P(),
            P(),
        ),
        out_specs=(P(("dp", "col"), "row"), P(("dp", "col"), None)),
        check_vma=False,
    )
```
